32 devices in a mesh: groups: 2 (over y), sec: 4 (over z), strip: 2 (over x), chan: 2 (over core).
Axes of the slice: x: 2, y: 2, z: 4, core: 2. Of those that a mesh axis runs over, the one named last changes fastest.
Arguments:
- sections: bfloat16 [16, 16, 1024], P(('groups', 'sec'), 'strip'), parts along dimension 0, may hold values from -64 to 64
- w_first: bfloat16 [32, 9], replicated, may hold values from -2 to 2
- w_second: bfloat16 [9, 32, 32], replicated, may hold values from -0.375 to 0.375
- offsets: int32 [16, 2, 16, 1024], P(('groups', 'sec'), None, 'strip'), parts along dimension 0, may hold values from -32 to 31
Outputs:
- warped: bfloat16 [16, 32, 16, 1024], P(('groups', 'sec'), 'chan', 'strip'), parts along dimension 0
- composed: float32 [16, 2, 16, 1024], P(('groups', 'sec'), None, 'strip'), parts along dimension 0
The draws below stay inside these ranges and needn't reach their ends.
There are 2 independent parts, one for each index of `groups`. The reference program is written for one: setup_inputs(seed, part) draws one part's arguments, and reference() takes and returns one part's arrays. A program takes and returns all parts, laid end to end along the dimension named above; an argument that names none is the same for every part. Nothing has to cross between parts.
All inputs are finite; a program needn't handle non-finite values.
Results may differ from the reference program's by a relative error of at most 0.0083.
Values may be sent and summed in bfloat16 or wider, within the bound.
No kernel may reach another device: no remote copies, remote signals or barrier semaphores. Data moves between devices by JAX's collectives and lax.ppermute only.
A program may use at most 64 MiB of HBM per device.

```python
import jax
import jax.numpy as jnp
from jax import lax

W = 1024
C = 32
HEAD_CH = 16
SECTIONS = 8
ROWS = 16
N_CHAN = 2


def draw_sections(key, part):
    base_draw = jax.random.normal(key, (SECTIONS, ROWS, W), jnp.float32)
    return jnp.clip(base_draw, -6.0, 6.0).astype(jnp.bfloat16)


def touch_ends(entries, stream_key, smallest, largest):
    place = [jax.random.randint(jax.random.fold_in(stream_key, axis), (), 0, length) for axis, length in enumerate(entries.shape)]
    main_axis = entries.shape.index(max(entries.shape))
    neighbour = place[:main_axis] + [(place[main_axis] + 1) % entries.shape[main_axis]] + place[main_axis + 1:]
    return entries.at[tuple(place)].set(smallest).at[tuple(neighbour)].set(largest)


def noise(key, shape, deviation, reach, held_as=jnp.bfloat16):
    return jnp.clip(deviation * jax.random.normal(key, shape, jnp.float32), -reach, reach).astype(held_as)


def setup_inputs(seed: int = 0, part: int = 0) -> dict:
    streams_of = jax.random.split(jax.random.key(seed), 5)
    own_keys = jax.random.split(jax.random.fold_in(streams_of[4], part), 5)
    sections = draw_sections(jax.random.fold_in(jax.random.fold_in(streams_of[4], part), 71), part)
    w_first = noise(streams_of[1], (C, 9), 9 ** -0.5, 2.0)
    w_second = noise(streams_of[2], (9, C, C), (9 * C) ** -0.5, 0.375)
    offsets = touch_ends(jax.random.randint(own_keys[3], (SECTIONS, 2, ROWS, W), -32, 32), jax.random.fold_in(own_keys[3], 1), -32, 31).astype(jnp.int32)
    return {"sections": sections, "w_first": w_first, "w_second": w_second, "offsets": offsets}


score_scale = 4.0


def first_taps(extended, rows_out, row_start):
    columns = extended.shape[-1]
    padded = jnp.pad(extended, ((0, 0), (0, 0), (2, 2)))
    tap_list = []
    for shift_y in (-2, 0, 2):
        for shift_x in (-2, 0, 2):
            tap_list.append(padded[:, row_start + shift_y:row_start + shift_y + rows_out, 2 + shift_x:2 + shift_x + columns])
    return jnp.stack(tap_list)


def second_terms(weights, inputs):
    rows_out = inputs.shape[2] - 2
    columns = inputs.shape[3]
    padded = jnp.pad(inputs, ((0, 0), (0, 0), (0, 0), (1, 1))).astype(jnp.float32)
    weights = weights.astype(jnp.float32)
    summed = None
    tap_index = 0
    for shift_y in (-1, 0, 1):
        for shift_x in (-1, 0, 1):
            window = padded[:, :, 1 + shift_y:1 + shift_y + rows_out, 1 + shift_x:1 + shift_x + columns]
            tap_term = jnp.einsum("oi,ispw->ospw", weights[tap_index], window, precision=lax.Precision.HIGHEST)
            summed = tap_term if summed is None else summed + tap_term
            tap_index += 1
    return summed


def sample(source, quant, row_start):
    channel_count, rows_in, width_pad = source.shape
    rows_out, columns = quant.shape[1], quant.shape[2]
    base_y = jnp.floor_divide(quant[0], 8)
    frac_y = (quant[0] - 8 * base_y).astype(jnp.float32) * 0.125
    base_x = jnp.floor_divide(quant[1], 8)
    frac_x = (quant[1] - 8 * base_x).astype(jnp.float32) * 0.125
    flat_source = source.reshape(channel_count, rows_in * width_pad)
    row_ids = lax.broadcasted_iota(jnp.int32, (rows_out, columns), 0) + row_start + base_y
    col_ids = lax.broadcasted_iota(jnp.int32, (rows_out, columns), 1) + 4 + base_x
    summed = jnp.zeros((channel_count, rows_out, columns), jnp.float32)
    for step_y, weight_y in ((0, 1.0 - frac_y), (1, frac_y)):
        for step_x, weight_x in ((0, 1.0 - frac_x), (1, frac_x)):
            flat_index = ((row_ids + step_y) * width_pad + col_ids + step_x).reshape(-1).astype(jnp.int32)
            values = jnp.take(flat_source, flat_index, axis=1).reshape(channel_count, rows_out, columns).astype(jnp.float32)
            summed = summed + (weight_y * weight_x) * values
    return summed


def reference(sections, w_first, w_second, offsets):
    def features_of(section):
        extended = jnp.pad(section, ((2, 2), (0, 0)))[None]
        tap_stack = first_taps(extended, ROWS, 2).astype(jnp.float32)
        first_maps = jnp.einsum("ct,tspw->cspw", w_first.astype(jnp.float32), tap_stack, precision=lax.Precision.HIGHEST)
        first_maps = jnp.maximum(first_maps, 0.0).astype(jnp.bfloat16)
        padded_rows = jnp.pad(first_maps, ((0, 0), (0, 0), (1, 1), (0, 0)))
        mixed_sum = second_terms(w_second, padded_rows)
        return jnp.maximum(mixed_sum, 0.0).astype(jnp.bfloat16)[:, 0]

    features = lax.map(features_of, sections)
    disp_y = (jnp.arange(81) // 9 - 4).astype(jnp.float32)[:, None, None]
    disp_x = (jnp.arange(81) % 9 - 4).astype(jnp.float32)[:, None, None]

    def flow_of(position):
        current = lax.dynamic_index_in_dim(features, position, 0, keepdims=False).astype(jnp.float32)
        earlier = lax.dynamic_index_in_dim(features, jnp.maximum(position - 1, 0).astype(jnp.int32), 0, keepdims=False).astype(jnp.float32)
        earlier = jnp.where(position > 0, earlier, jnp.zeros_like(earlier))
        padded = jnp.pad(earlier, ((0, 0), (4, 4), (4, 4)))
        summed = jnp.zeros((2, ROWS, W), jnp.float32)
        for head_index in range(N_CHAN):
            cur_head = current[head_index * HEAD_CH:(head_index + 1) * HEAD_CH]
            pad_head = padded[head_index * HEAD_CH:(head_index + 1) * HEAD_CH]
            scores = jnp.stack([jnp.sum(cur_head * pad_head[:, shift_y:shift_y + ROWS, shift_x:shift_x + W], axis=0)
                                for shift_y in range(9) for shift_x in range(9)]) * (score_scale / HEAD_CH)
            probs = jax.nn.softmax(scores, axis=0)
            summed = summed + jnp.stack([jnp.sum(probs * disp_y, axis=0), jnp.sum(probs * disp_x, axis=0)])
        return summed / N_CHAN

    flow_field = lax.map(flow_of, jnp.arange(SECTIONS).astype(jnp.int32))

    def warp_of(pair):
        section_features, quant = pair
        padded = jnp.pad(section_features, ((0, 0), (4, 4), (4, 4)))
        return sample(padded, quant, 4).astype(jnp.bfloat16)

    warped = lax.map(warp_of, (features, offsets))

    def compose_step(previous, pair):
        flow_now, quant = pair
        padded = jnp.pad(previous, ((0, 0), (4, 4), (4, 4)))
        current = flow_now + quant.astype(jnp.float32) * 0.125 + sample(padded, quant, 4)
        return current, current

    composed = lax.scan(compose_step, jnp.zeros((2, ROWS, W), jnp.float32), (flow_field, offsets))[1]
    return (warped, composed)
```

```python
import jax
import jax.numpy as jnp
from jax import lax
from jax.sharding import PartitionSpec as P

score_scale = 4.0


def shifted_from(value, axes, sizes, deltas, cyclic=False):
    pairs = []
    counts = [int(s) for s in sizes]
    total = 1
    for c in counts:
        total *= c
    for dst in range(total):
        coords = []
        rem = dst
        for c in reversed(counts):
            coords.append(rem % c)
            rem //= c
        coords = coords[::-1]
        src_coords = []
        ok = True
        for coord, c, d in zip(coords, counts, deltas):
            s = coord - d
            if cyclic:
                s %= c
            elif s < 0 or s >= c:
                ok = False
            src_coords.append(s)
        if not ok:
            continue
        src = 0
        for s, c in zip(src_coords, counts):
            src = src * c + s
        if src != dst:
            pairs.append((src, dst))
    if not pairs:
        return jnp.zeros_like(value)
    return lax.ppermute(value, axes if len(axes) > 1 else axes[0], pairs)


def first_taps(extended, rows_out, row_start):
    columns = extended.shape[-1]
    padded = jnp.pad(extended, ((0, 0), (0, 0), (2, 2)))
    tap_list = []
    for shift_y in (-2, 0, 2):
        for shift_x in (-2, 0, 2):
            tap_list.append(
                padded[
                    :,
                    row_start + shift_y : row_start + shift_y + rows_out,
                    2 + shift_x : 2 + shift_x + columns,
                ]
            )
    return jnp.stack(tap_list)


def second_terms(weights, inputs):
    rows_out = inputs.shape[2] - 2
    columns = inputs.shape[3]
    padded = jnp.pad(inputs, ((0, 0), (0, 0), (0, 0), (1, 1)))
    summed = None
    tap_index = 0
    for shift_y in (-1, 0, 1):
        for shift_x in (-1, 0, 1):
            window = padded[
                :, :, 1 + shift_y : 1 + shift_y + rows_out, 1 + shift_x : 1 + shift_x + columns
            ]
            tap_term = jnp.einsum(
                "oi,ispw->ospw", weights[tap_index], window, preferred_element_type=jnp.float32
            )
            summed = tap_term if summed is None else summed + tap_term
            tap_index += 1
    return summed


def hat_weights(quant_row):
    base = jnp.floor_divide(quant_row, 8)
    frac = (quant_row - 8 * base).astype(jnp.float32) * 0.125
    return [
        jnp.where(base == shift, 1.0 - frac, 0.0) + jnp.where(base + 1 == shift, frac, 0.0)
        for shift in range(-4, 5)
    ]


def sample(source, quant, row_start):
    rows_out, columns = (quant.shape[1], quant.shape[2])
    hats_y = hat_weights(quant[0])
    hats_x = hat_weights(quant[1])
    summed = jnp.zeros((source.shape[0], rows_out, columns), jnp.float32)
    for index_x in range(9):
        inner = jnp.zeros((source.shape[0], rows_out, columns), jnp.float32)
        for index_y in range(9):
            lower = row_start + index_y - 4
            window = source[:, lower : lower + rows_out, index_x : index_x + columns].astype(
                jnp.float32
            )
            inner = inner + hats_y[index_y] * window
        summed = summed + hats_x[index_x] * inner
    return summed


def local(sections, w_first, w_second, offsets):
    sec_local, strip_rows, columns = sections.shape
    n_sec = lax.axis_size("sec")
    n_strip = lax.axis_size("strip")
    n_chan = lax.axis_size("chan")
    strip_index = lax.axis_index("strip")
    own_index = lax.axis_index("chan")
    head_width = w_second.shape[1] // n_chan
    strip_first = strip_index * strip_rows
    total_rows = strip_rows * n_strip
    halo = 7
    ss = ("sec", "strip")
    ss_sizes = (n_sec, n_strip)

    from_left = shifted_from(sections[:, strip_rows - halo :], ss, ss_sizes, (0, 1))
    from_right = shifted_from(sections[:, :halo], ss, ss_sizes, (0, -1))
    last = sections[sec_local - 1 :]
    behind = shifted_from(last, ss, ss_sizes, (1, 0))
    behind_left = shifted_from(last[:, strip_rows - halo :], ss, ss_sizes, (1, 1))
    behind_right = shifted_from(last[:, :halo], ss, ss_sizes, (1, -1))
    own_ext = jnp.concatenate([from_left, sections, from_right], axis=1)
    prev_ext = jnp.concatenate([behind_left, behind, behind_right], axis=1)
    all_ext = jnp.concatenate([prev_ext, own_ext], axis=0)

    offset_parts = [None] * n_strip
    offset_parts[0] = offsets
    for k in range(1, n_strip):
        offset_parts[k] = shifted_from(offsets, ("strip",), (n_strip,), (k,), cyclic=True)
    offset_rows = []
    for slot in range(n_strip):
        piece = offset_parts[0]
        for k in range(1, n_strip):
            piece = jnp.where((strip_index - k) % n_strip == slot, offset_parts[k], piece)
        offset_rows.append(piece)
    q_full = jnp.concatenate(offset_rows, axis=2)

    first_rows = strip_rows + 10
    tap_stack = first_taps(all_ext, first_rows, 2)
    global_rows = strip_first - 5 + lax.broadcasted_iota(jnp.int32, (first_rows, 1), 0)
    inside = (global_rows >= 0) & (global_rows < total_rows)
    all_maps = jnp.einsum("ct,tspw->cspw", w_first, tap_stack, preferred_element_type=jnp.float32)
    all_maps = jnp.where(inside, jnp.maximum(all_maps, 0.0), 0.0).astype(jnp.bfloat16)
    w_outputs = lax.dynamic_slice_in_dim(w_second, own_index * head_width, head_width, 1)
    mixed_sum = second_terms(w_outputs, all_maps)
    feat_rows = global_rows[1:-1]
    feat_inside = (feat_rows >= 0) & (feat_rows < total_rows)
    framed = jnp.where(feat_inside, jnp.maximum(mixed_sum, 0.0), 0.0).astype(jnp.bfloat16)

    current = framed[:, 1:, 4 : 4 + strip_rows, :]
    earlier = jnp.pad(framed[:, :sec_local], ((0, 0), (0, 0), (0, 0), (4, 4)))
    factor = score_scale / head_width
    field_shape = (sec_local, strip_rows, columns)
    running_max = jnp.full(field_shape, -1e30, jnp.float32)
    weight_sum = jnp.zeros(field_shape, jnp.float32)
    along_y = jnp.zeros(field_shape, jnp.float32)
    along_x = jnp.zeros(field_shape, jnp.float32)
    step_cols = lax.broadcasted_iota(jnp.float32, (9, 1, 1, 1), 0) - 4.0
    for shift_y in range(9):
        scores = (
            jnp.stack(
                [
                    jnp.einsum(
                        "cspw,cspw->spw",
                        current,
                        earlier[:, :, shift_y : shift_y + strip_rows, shift_x : shift_x + columns],
                        preferred_element_type=jnp.float32,
                    )
                    for shift_x in range(9)
                ]
            )
            * factor
        )
        highest = jnp.maximum(running_max, jnp.max(scores, axis=0))
        rescale = jnp.exp(running_max - highest)
        weights = jnp.exp(scores - highest)
        block_sum = jnp.sum(weights, axis=0)
        weight_sum = weight_sum * rescale + block_sum
        along_y = along_y * rescale + (shift_y - 4.0) * block_sum
        along_x = along_x * rescale + jnp.sum(weights * step_cols, axis=0)
        running_max = highest
    head_flow = jnp.stack([along_y / weight_sum, along_x / weight_sum], axis=1)

    sc = ("strip", "chan")
    sc_sizes = (n_strip, n_chan)
    flow_slots = [jnp.zeros_like(head_flow) for _ in range(n_strip)]
    for k in range(n_strip * n_chan):
        if k == 0:
            got = head_flow
        else:
            got = shifted_from(head_flow, sc, sc_sizes, (k // n_chan, k % n_chan), cyclic=True)
        src_strip = (strip_index - k // n_chan) % n_strip
        for slot in range(n_strip):
            flow_slots[slot] = flow_slots[slot] + jnp.where(src_strip == slot, got, 0.0)
    flows_full = jnp.concatenate(flow_slots, axis=2) / n_chan

    warped_list = []
    for local_sec in range(sec_local):
        source = jnp.pad(framed[:, local_sec + 1], ((0, 0), (0, 0), (4, 4)))
        warped_list.append(sample(source, offsets[local_sec], 4).astype(jnp.bfloat16))
    warped = jnp.stack(warped_list)

    base_terms = flows_full + q_full.astype(jnp.float32) * 0.125

    def chain_local(incoming):
        src = incoming
        outs = []
        for local_sec in range(sec_local):
            src = base_terms[local_sec] + sample(
                jnp.pad(src, ((0, 0), (4, 4), (4, 4))), q_full[local_sec], 4
            )
            outs.append(src)
        return outs

    outs = chain_local(jnp.zeros((2, total_rows, columns), jnp.float32))
    for turn in range(1, n_sec):
        incoming = shifted_from(outs[-1], ("sec",), (n_sec,), (1,))
        outs = chain_local(incoming)
    composed = jnp.stack(
        [lax.dynamic_slice_in_dim(o, strip_first, strip_rows, 1) for o in outs]
    )
    return (warped, composed)


def solution(mesh):
    in_specs = (
        P(("groups", "sec"), "strip", None),
        P(),
        P(),
        P(("groups", "sec"), None, "strip", None),
    )
    out_specs = (
        P(("groups", "sec"), "chan", "strip", None),
        P(("groups", "sec"), None, "strip", None),
    )
    return jax.shard_map(local, mesh=mesh, in_specs=in_specs, out_specs=out_specs, check_vma=False)
```

```python
import jax
import jax.numpy as jnp
from jax import lax
from jax.sharding import PartitionSpec as P

score_scale = 4.0


def shifted_from(value, axes, sizes, deltas, cyclic=False):
    pairs = []
    counts = [int(s) for s in sizes]
    total = 1
    for c in counts:
        total *= c
    for dst in range(total):
        coords = []
        rem = dst
        for c in reversed(counts):
            coords.append(rem % c)
            rem //= c
        coords = coords[::-1]
        src_coords = []
        ok = True
        for coord, c, d in zip(coords, counts, deltas):
            s = coord - d
            if cyclic:
                s %= c
            elif s < 0 or s >= c:
                ok = False
            src_coords.append(s)
        if not ok:
            continue
        src = 0
        for s, c in zip(src_coords, counts):
            src = src * c + s
        if src != dst:
            pairs.append((src, dst))
    if not pairs:
        return jnp.zeros_like(value)
    return lax.ppermute(value, axes if len(axes) > 1 else axes[0], pairs)


def first_taps(extended, rows_out, row_start):
    columns = extended.shape[-1]
    padded = jnp.pad(extended, ((0, 0), (0, 0), (2, 2)))
    tap_list = []
    for shift_y in (-2, 0, 2):
        for shift_x in (-2, 0, 2):
            tap_list.append(
                padded[
                    :,
                    row_start + shift_y : row_start + shift_y + rows_out,
                    2 + shift_x : 2 + shift_x + columns,
                ]
            )
    return jnp.stack(tap_list)


def second_terms(weights, inputs):
    rows_out = inputs.shape[2] - 2
    columns = inputs.shape[3]
    padded = jnp.pad(inputs, ((0, 0), (0, 0), (0, 0), (1, 1)))
    summed = None
    tap_index = 0
    for shift_y in (-1, 0, 1):
        for shift_x in (-1, 0, 1):
            window = padded[
                :, :, 1 + shift_y : 1 + shift_y + rows_out, 1 + shift_x : 1 + shift_x + columns
            ]
            tap_term = jnp.einsum(
                "oi,ispw->ospw", weights[tap_index], window, preferred_element_type=jnp.float32
            )
            summed = tap_term if summed is None else summed + tap_term
            tap_index += 1
    return summed


def hat_weights(quant_row):
    base = jnp.floor_divide(quant_row, 8)
    frac = (quant_row - 8 * base).astype(jnp.float32) * 0.125
    return [
        jnp.where(base == shift, 1.0 - frac, 0.0) + jnp.where(base + 1 == shift, frac, 0.0)
        for shift in range(-4, 5)
    ]


def sample(source, quant, row_start):
    rows_out, columns = (quant.shape[1], quant.shape[2])
    hats_y = hat_weights(quant[0])
    hats_x = hat_weights(quant[1])
    summed = jnp.zeros((source.shape[0], rows_out, columns), jnp.float32)
    for index_x in range(9):
        inner = jnp.zeros((source.shape[0], rows_out, columns), jnp.float32)
        for index_y in range(9):
            lower = row_start + index_y - 4
            window = source[:, lower : lower + rows_out, index_x : index_x + columns].astype(
                jnp.float32
            )
            inner = inner + hats_y[index_y] * window
        summed = summed + hats_x[index_x] * inner
    return summed


def local(sections, w_first, w_second, offsets):
    sec_local, strip_rows, columns = sections.shape
    n_sec = lax.axis_size("sec")
    n_strip = lax.axis_size("strip")
    n_chan = lax.axis_size("chan")
    strip_index = lax.axis_index("strip")
    own_index = lax.axis_index("chan")
    head_width = w_second.shape[1] // n_chan
    strip_first = strip_index * strip_rows
    total_rows = strip_rows * n_strip
    halo = 7
    ss = ("sec", "strip")
    ss_sizes = (n_sec, n_strip)

    if n_strip == 2:
        packed = jnp.concatenate(
            [sections[:, None].astype(jnp.float32), offsets.astype(jnp.float32)], axis=1
        ).astype(jnp.bfloat16)
        partner = shifted_from(packed, ("strip",), (n_strip,), (1,), cyclic=True)
        other_sec = partner[:, 0]
        from_left = jnp.where(strip_index == 1, other_sec[:, strip_rows - halo :], 0.0)
        from_right = jnp.where(strip_index == 0, other_sec[:, :halo], 0.0)
        other_q = partner[:, 1:].astype(jnp.int32)
        q_full = jnp.where(
            strip_index == 0,
            jnp.concatenate([offsets, other_q], axis=2),
            jnp.concatenate([other_q, offsets], axis=2),
        )
    else:
        from_left = shifted_from(sections[:, strip_rows - halo :], ("strip",), (n_strip,), (1,))
        from_right = shifted_from(sections[:, :halo], ("strip",), (n_strip,), (-1,))
        offset_parts = [offsets]
        for k in range(1, n_strip):
            offset_parts.append(shifted_from(offsets, ("strip",), (n_strip,), (k,), cyclic=True))
        offset_rows = []
        for slot in range(n_strip):
            piece = offset_parts[0]
            for k in range(1, n_strip):
                piece = jnp.where((strip_index - k) % n_strip == slot, offset_parts[k], piece)
            offset_rows.append(piece)
        q_full = jnp.concatenate(offset_rows, axis=2)
    own_ext = jnp.concatenate([from_left, sections, from_right], axis=1)
    prev_ext = shifted_from(own_ext[sec_local - 1 :], ("sec",), (n_sec,), (1,))

    first_rows = strip_rows + 10
    global_rows = strip_first - 5 + lax.broadcasted_iota(jnp.int32, (first_rows, 1), 0)
    inside = (global_rows >= 0) & (global_rows < total_rows)
    feat_rows = global_rows[1:-1]
    feat_inside = (feat_rows >= 0) & (feat_rows < total_rows)
    k_first = w_first.reshape(w_first.shape[0], 1, 3, 3)
    w_outputs = lax.dynamic_slice_in_dim(w_second, own_index * head_width, head_width, 1)
    k_second = w_outputs.reshape(3, 3, head_width, w_second.shape[2]).transpose(2, 3, 0, 1)
    dims = ("NCHW", "OIHW", "NCHW")

    def features_of(ext):
        maps = lax.conv_general_dilated(
            ext[:, None], k_first, (1, 1), ((0, 0), (2, 2)), rhs_dilation=(2, 2),
            dimension_numbers=dims, preferred_element_type=jnp.float32,
        )
        maps = jnp.where(inside, jnp.maximum(maps, 0.0), 0.0).astype(jnp.bfloat16)
        mixed = lax.conv_general_dilated(
            maps, k_second, (1, 1), ((0, 0), (1, 1)),
            dimension_numbers=dims, preferred_element_type=jnp.float32,
        )
        return jnp.where(feat_inside, jnp.maximum(mixed, 0.0), 0.0).astype(jnp.bfloat16)

    own_feat = features_of(own_ext)
    prev_feat = features_of(prev_ext)
    framed = jnp.concatenate([prev_feat, own_feat], axis=0).transpose(1, 0, 2, 3)

    current = framed[:, 1:, 4 : 4 + strip_rows, :]
    earlier = jnp.pad(framed[:, :sec_local], ((0, 0), (0, 0), (0, 0), (4, 4)))
    factor = score_scale / head_width
    field_shape = (sec_local, strip_rows, columns)
    running_max = jnp.full(field_shape, -1e30, jnp.float32)
    weight_sum = jnp.zeros(field_shape, jnp.float32)
    along_y = jnp.zeros(field_shape, jnp.float32)
    along_x = jnp.zeros(field_shape, jnp.float32)
    step_cols = lax.broadcasted_iota(jnp.float32, (9, 1, 1, 1), 0) - 4.0
    for shift_y in range(9):
        scores = (
            jnp.stack(
                [
                    jnp.einsum(
                        "cspw,cspw->spw",
                        current,
                        earlier[:, :, shift_y : shift_y + strip_rows, shift_x : shift_x + columns],
                        preferred_element_type=jnp.float32,
                    )
                    for shift_x in range(9)
                ]
            )
            * factor
        )
        highest = jnp.maximum(running_max, jnp.max(scores, axis=0))
        rescale = jnp.exp(running_max - highest)
        weights = jnp.exp(scores - highest)
        block_sum = jnp.sum(weights, axis=0)
        weight_sum = weight_sum * rescale + block_sum
        along_y = along_y * rescale + (shift_y - 4.0) * block_sum
        along_x = along_x * rescale + jnp.sum(weights * step_cols, axis=0)
        running_max = highest
    head_flow = jnp.stack([along_y / weight_sum, along_x / weight_sum], axis=1)

    sc = ("strip", "chan")
    sc_sizes = (n_strip, n_chan)
    flow_slots = [jnp.zeros_like(head_flow) for _ in range(n_strip)]
    for k in range(n_strip * n_chan):
        if k == 0:
            got = head_flow
        else:
            got = shifted_from(head_flow, sc, sc_sizes, (k // n_chan, k % n_chan), cyclic=True)
        src_strip = (strip_index - k // n_chan) % n_strip
        for slot in range(n_strip):
            flow_slots[slot] = flow_slots[slot] + jnp.where(src_strip == slot, got, 0.0)
    flows_full = jnp.concatenate(flow_slots, axis=2) / n_chan

    warped_list = []
    for local_sec in range(sec_local):
        source = jnp.pad(framed[:, local_sec + 1], ((0, 0), (0, 0), (4, 4)))
        warped_list.append(sample(source, offsets[local_sec], 4).astype(jnp.bfloat16))
    warped = jnp.stack(warped_list)

    base_terms = flows_full + q_full.astype(jnp.float32) * 0.125

    def chain_local(incoming):
        src = incoming
        outs = []
        for local_sec in range(sec_local):
            src = base_terms[local_sec] + sample(
                jnp.pad(src, ((0, 0), (4, 4), (4, 4))), q_full[local_sec], 4
            )
            outs.append(src)
        return outs

    outs = chain_local(jnp.zeros((2, total_rows, columns), jnp.float32))
    for turn in range(1, n_sec):
        incoming = shifted_from(outs[-1], ("sec",), (n_sec,), (1,))
        outs = chain_local(incoming)
    composed = jnp.stack(
        [lax.dynamic_slice_in_dim(o, strip_first, strip_rows, 1) for o in outs]
    )
    return (warped, composed)


def solution(mesh):
    in_specs = (
        P(("groups", "sec"), "strip", None),
        P(),
        P(),
        P(("groups", "sec"), None, "strip", None),
    )
    out_specs = (
        P(("groups", "sec"), "chan", "strip", None),
        P(("groups", "sec"), None, "strip", None),
    )
    return jax.shard_map(local, mesh=mesh, in_specs=in_specs, out_specs=out_specs, check_vma=False)
```

```python
import jax
import jax.numpy as jnp
from jax import lax
from jax.sharding import PartitionSpec as P

score_scale = 4.0


def shifted_from(value, axes, sizes, deltas, cyclic=False):
    pairs = []
    counts = [int(s) for s in sizes]
    total = 1
    for c in counts:
        total *= c
    for dst in range(total):
        coords = []
        rem = dst
        for c in reversed(counts):
            coords.append(rem % c)
            rem //= c
        coords = coords[::-1]
        src_coords = []
        ok = True
        for coord, c, d in zip(coords, counts, deltas):
            s = coord - d
            if cyclic:
                s %= c
            elif s < 0 or s >= c:
                ok = False
            src_coords.append(s)
        if not ok:
            continue
        src = 0
        for s, c in zip(src_coords, counts):
            src = src * c + s
        if src != dst:
            pairs.append((src, dst))
    if not pairs:
        return jnp.zeros_like(value)
    return lax.ppermute(value, axes if len(axes) > 1 else axes[0], pairs)


def first_taps(extended, rows_out, row_start):
    columns = extended.shape[-1]
    padded = jnp.pad(extended, ((0, 0), (0, 0), (2, 2)))
    tap_list = []
    for shift_y in (-2, 0, 2):
        for shift_x in (-2, 0, 2):
            tap_list.append(
                padded[
                    :,
                    row_start + shift_y : row_start + shift_y + rows_out,
                    2 + shift_x : 2 + shift_x + columns,
                ]
            )
    return jnp.stack(tap_list)


def second_terms(weights, inputs):
    rows_out = inputs.shape[2] - 2
    columns = inputs.shape[3]
    padded = jnp.pad(inputs, ((0, 0), (0, 0), (0, 0), (1, 1)))
    summed = None
    tap_index = 0
    for shift_y in (-1, 0, 1):
        for shift_x in (-1, 0, 1):
            window = padded[
                :, :, 1 + shift_y : 1 + shift_y + rows_out, 1 + shift_x : 1 + shift_x + columns
            ]
            tap_term = jnp.einsum(
                "oi,ispw->ospw", weights[tap_index], window, preferred_element_type=jnp.float32
            )
            summed = tap_term if summed is None else summed + tap_term
            tap_index += 1
    return summed


def hat_weights(quant_row):
    base = jnp.floor_divide(quant_row, 8)
    frac = (quant_row - 8 * base).astype(jnp.float32) * 0.125
    return [
        jnp.where(base == shift, 1.0 - frac, 0.0) + jnp.where(base + 1 == shift, frac, 0.0)
        for shift in range(-4, 5)
    ]


def sample(source, quant, row_start):
    rows_out, columns = (quant.shape[1], quant.shape[2])
    hats_y = hat_weights(quant[0])
    hats_x = hat_weights(quant[1])
    summed = jnp.zeros((source.shape[0], rows_out, columns), jnp.float32)
    for index_x in range(9):
        inner = jnp.zeros((source.shape[0], rows_out, columns), jnp.float32)
        for index_y in range(9):
            lower = row_start + index_y - 4
            window = source[:, lower : lower + rows_out, index_x : index_x + columns].astype(
                jnp.float32
            )
            inner = inner + hats_y[index_y] * window
        summed = summed + hats_x[index_x] * inner
    return summed


def local(sections, w_first, w_second, offsets):
    sec_local, strip_rows, columns = sections.shape
    n_sec = lax.axis_size("sec")
    n_strip = lax.axis_size("strip")
    n_chan = lax.axis_size("chan")
    strip_index = lax.axis_index("strip")
    own_index = lax.axis_index("chan")
    head_width = w_second.shape[1] // n_chan
    strip_first = strip_index * strip_rows
    total_rows = strip_rows * n_strip
    halo = 7
    ss = ("sec", "strip")
    ss_sizes = (n_sec, n_strip)

    if n_strip == 2:
        packed = jnp.concatenate(
            [sections[:, None].astype(jnp.float32), offsets.astype(jnp.float32)], axis=1
        ).astype(jnp.bfloat16)
        partner = shifted_from(packed, ("strip",), (n_strip,), (1,), cyclic=True)
        other_sec = partner[:, 0]
        from_left = jnp.where(strip_index == 1, other_sec[:, strip_rows - halo :], 0.0)
        from_right = jnp.where(strip_index == 0, other_sec[:, :halo], 0.0)
        other_q = partner[:, 1:].astype(jnp.int32)
        q_full = jnp.where(
            strip_index == 0,
            jnp.concatenate([offsets, other_q], axis=2),
            jnp.concatenate([other_q, offsets], axis=2),
        )
    else:
        from_left = shifted_from(sections[:, strip_rows - halo :], ("strip",), (n_strip,), (1,))
        from_right = shifted_from(sections[:, :halo], ("strip",), (n_strip,), (-1,))
        offset_parts = [offsets]
        for k in range(1, n_strip):
            offset_parts.append(shifted_from(offsets, ("strip",), (n_strip,), (k,), cyclic=True))
        offset_rows = []
        for slot in range(n_strip):
            piece = offset_parts[0]
            for k in range(1, n_strip):
                piece = jnp.where((strip_index - k) % n_strip == slot, offset_parts[k], piece)
            offset_rows.append(piece)
        q_full = jnp.concatenate(offset_rows, axis=2)
    own_ext = jnp.concatenate([from_left, sections, from_right], axis=1)
    prev_ext = shifted_from(own_ext[sec_local - 1 :], ("sec",), (n_sec,), (1,))

    first_rows = strip_rows + 10
    global_rows = strip_first - 5 + lax.broadcasted_iota(jnp.int32, (first_rows, 1), 0)
    inside = (global_rows >= 0) & (global_rows < total_rows)
    feat_rows = global_rows[1:-1]
    feat_inside = (feat_rows >= 0) & (feat_rows < total_rows)
    w_outputs = lax.dynamic_slice_in_dim(w_second, own_index * head_width, head_width, 1)
    w_taps = w_first.astype(jnp.float32)

    def features_of(ext):
        padded = jnp.pad(ext, ((0, 0), (0, 0), (2, 2))).astype(jnp.float32)
        maps = None
        tap_index = 0
        for shift_y in (-2, 0, 2):
            for shift_x in (-2, 0, 2):
                window = padded[:, 2 + shift_y : 2 + shift_y + first_rows, 2 + shift_x : 2 + shift_x + columns]
                term = w_taps[:, tap_index, None, None, None] * window[None]
                maps = term if maps is None else maps + term
                tap_index += 1
        maps = jnp.where(inside, jnp.maximum(maps, 0.0), 0.0).astype(jnp.bfloat16)
        mixed = second_terms(w_outputs, maps)
        return jnp.where(feat_inside, jnp.maximum(mixed, 0.0), 0.0).astype(jnp.bfloat16)

    framed = features_of(jnp.concatenate([prev_ext, own_ext], axis=0))

    current = framed[:, 1:, 4 : 4 + strip_rows, :]
    earlier = jnp.pad(framed[:, :sec_local], ((0, 0), (0, 0), (0, 0), (4, 4)))
    factor = score_scale / head_width
    field_shape = (sec_local, strip_rows, columns)
    running_max = jnp.full(field_shape, -1e30, jnp.float32)
    weight_sum = jnp.zeros(field_shape, jnp.float32)
    along_y = jnp.zeros(field_shape, jnp.float32)
    along_x = jnp.zeros(field_shape, jnp.float32)
    step_cols = lax.broadcasted_iota(jnp.float32, (9, 1, 1, 1), 0) - 4.0
    for shift_y in range(9):
        scores = (
            jnp.stack(
                [
                    jnp.einsum(
                        "cspw,cspw->spw",
                        current,
                        earlier[:, :, shift_y : shift_y + strip_rows, shift_x : shift_x + columns],
                        preferred_element_type=jnp.float32,
                    )
                    for shift_x in range(9)
                ]
            )
            * factor
        )
        highest = jnp.maximum(running_max, jnp.max(scores, axis=0))
        rescale = jnp.exp(running_max - highest)
        weights = jnp.exp(scores - highest)
        block_sum = jnp.sum(weights, axis=0)
        weight_sum = weight_sum * rescale + block_sum
        along_y = along_y * rescale + (shift_y - 4.0) * block_sum
        along_x = along_x * rescale + jnp.sum(weights * step_cols, axis=0)
        running_max = highest
    head_flow = jnp.stack([along_y / weight_sum, along_x / weight_sum], axis=1)

    sc = ("strip", "chan")
    sc_sizes = (n_strip, n_chan)
    flow_slots = [jnp.zeros_like(head_flow) for _ in range(n_strip)]
    for k in range(n_strip * n_chan):
        if k == 0:
            got = head_flow
        else:
            got = shifted_from(head_flow, sc, sc_sizes, (k // n_chan, k % n_chan), cyclic=True)
        src_strip = (strip_index - k // n_chan) % n_strip
        for slot in range(n_strip):
            flow_slots[slot] = flow_slots[slot] + jnp.where(src_strip == slot, got, 0.0)
    flows_full = jnp.concatenate(flow_slots, axis=2) / n_chan

    warped_list = []
    for local_sec in range(sec_local):
        source = jnp.pad(framed[:, local_sec + 1], ((0, 0), (0, 0), (4, 4)))
        warped_list.append(sample(source, offsets[local_sec], 4).astype(jnp.bfloat16))
    warped = jnp.stack(warped_list)

    base_terms = flows_full + q_full.astype(jnp.float32) * 0.125

    def chain_local(incoming):
        src = incoming
        outs = []
        for local_sec in range(sec_local):
            src = base_terms[local_sec] + sample(
                jnp.pad(src, ((0, 0), (4, 4), (4, 4))), q_full[local_sec], 4
            )
            outs.append(src)
        return outs

    outs = chain_local(jnp.zeros((2, total_rows, columns), jnp.float32))
    for turn in range(1, n_sec):
        incoming = shifted_from(outs[-1], ("sec",), (n_sec,), (1,))
        outs = chain_local(incoming)
    composed = jnp.stack(
        [lax.dynamic_slice_in_dim(o, strip_first, strip_rows, 1) for o in outs]
    )
    return (warped, composed)


def solution(mesh):
    in_specs = (
        P(("groups", "sec"), "strip", None),
        P(),
        P(),
        P(("groups", "sec"), None, "strip", None),
    )
    out_specs = (
        P(("groups", "sec"), "chan", "strip", None),
        P(("groups", "sec"), None, "strip", None),
    )
    return jax.shard_map(local, mesh=mesh, in_specs=in_specs, out_specs=out_specs, check_vma=False)
```

```python
import jax
import jax.numpy as jnp
from jax import lax
from jax.sharding import PartitionSpec as P

score_scale = 4.0


def shifted_from(value, axes, sizes, deltas, cyclic=False):
    pairs = []
    counts = [int(s) for s in sizes]
    total = 1
    for c in counts:
        total *= c
    for dst in range(total):
        coords = []
        rem = dst
        for c in reversed(counts):
            coords.append(rem % c)
            rem //= c
        coords = coords[::-1]
        src_coords = []
        ok = True
        for coord, c, d in zip(coords, counts, deltas):
            s = coord - d
            if cyclic:
                s %= c
            elif s < 0 or s >= c:
                ok = False
            src_coords.append(s)
        if not ok:
            continue
        src = 0
        for s, c in zip(src_coords, counts):
            src = src * c + s
        if src != dst:
            pairs.append((src, dst))
    if not pairs:
        return jnp.zeros_like(value)
    return lax.ppermute(value, axes if len(axes) > 1 else axes[0], pairs)


def first_taps(extended, rows_out, row_start):
    columns = extended.shape[-1]
    padded = jnp.pad(extended, ((0, 0), (0, 0), (2, 2)))
    tap_list = []
    for shift_y in (-2, 0, 2):
        for shift_x in (-2, 0, 2):
            tap_list.append(
                padded[
                    :,
                    row_start + shift_y : row_start + shift_y + rows_out,
                    2 + shift_x : 2 + shift_x + columns,
                ]
            )
    return jnp.stack(tap_list)


def second_terms(weights, inputs):
    rows_out = inputs.shape[2] - 2
    columns = inputs.shape[3]
    padded = jnp.pad(inputs, ((0, 0), (0, 0), (0, 0), (1, 1)))
    summed = None
    tap_index = 0
    for shift_y in (-1, 0, 1):
        for shift_x in (-1, 0, 1):
            window = padded[
                :, :, 1 + shift_y : 1 + shift_y + rows_out, 1 + shift_x : 1 + shift_x + columns
            ]
            tap_term = jnp.einsum(
                "oi,ispw->ospw", weights[tap_index], window, preferred_element_type=jnp.float32
            )
            summed = tap_term if summed is None else summed + tap_term
            tap_index += 1
    return summed


def hat_weights(quant_row):
    base = jnp.floor_divide(quant_row, 8)
    frac = (quant_row - 8 * base).astype(jnp.float32) * 0.125
    return [
        jnp.where(base == shift, 1.0 - frac, 0.0) + jnp.where(base + 1 == shift, frac, 0.0)
        for shift in range(-4, 5)
    ]


def sample(source, quant, row_start):
    rows_out, columns = (quant.shape[1], quant.shape[2])
    hats_y = hat_weights(quant[0])
    hats_x = hat_weights(quant[1])
    summed = jnp.zeros((source.shape[0], rows_out, columns), jnp.float32)
    for index_x in range(9):
        inner = jnp.zeros((source.shape[0], rows_out, columns), jnp.float32)
        for index_y in range(9):
            lower = row_start + index_y - 4
            window = source[:, lower : lower + rows_out, index_x : index_x + columns].astype(
                jnp.float32
            )
            inner = inner + hats_y[index_y] * window
        summed = summed + hats_x[index_x] * inner
    return summed


def local(sections, w_first, w_second, offsets):
    sec_local, strip_rows, columns = sections.shape
    n_sec = lax.axis_size("sec")
    n_strip = lax.axis_size("strip")
    n_chan = lax.axis_size("chan")
    strip_index = lax.axis_index("strip")
    own_index = lax.axis_index("chan")
    head_width = w_second.shape[1] // n_chan
    strip_first = strip_index * strip_rows
    total_rows = strip_rows * n_strip
    halo = 7
    ss = ("sec", "strip")
    ss_sizes = (n_sec, n_strip)

    if n_strip == 2:
        packed = jnp.concatenate(
            [sections[:, None].astype(jnp.float32), offsets.astype(jnp.float32)], axis=1
        ).astype(jnp.bfloat16)
        partner = shifted_from(packed, ("strip",), (n_strip,), (1,), cyclic=True)
        other_sec = partner[:, 0]
        from_left = jnp.where(strip_index == 1, other_sec[:, strip_rows - halo :], 0.0)
        from_right = jnp.where(strip_index == 0, other_sec[:, :halo], 0.0)
        other_q = partner[:, 1:].astype(jnp.int32)
        q_full = jnp.where(
            strip_index == 0,
            jnp.concatenate([offsets, other_q], axis=2),
            jnp.concatenate([other_q, offsets], axis=2),
        )
    else:
        from_left = shifted_from(sections[:, strip_rows - halo :], ("strip",), (n_strip,), (1,))
        from_right = shifted_from(sections[:, :halo], ("strip",), (n_strip,), (-1,))
        offset_parts = [offsets]
        for k in range(1, n_strip):
            offset_parts.append(shifted_from(offsets, ("strip",), (n_strip,), (k,), cyclic=True))
        offset_rows = []
        for slot in range(n_strip):
            piece = offset_parts[0]
            for k in range(1, n_strip):
                piece = jnp.where((strip_index - k) % n_strip == slot, offset_parts[k], piece)
            offset_rows.append(piece)
        q_full = jnp.concatenate(offset_rows, axis=2)
    own_ext = jnp.concatenate([from_left, sections, from_right], axis=1)
    prev_ext = shifted_from(own_ext[sec_local - 1 :], ("sec",), (n_sec,), (1,))

    first_rows = strip_rows + 10
    global_rows = strip_first - 5 + lax.broadcasted_iota(jnp.int32, (first_rows, 1), 0)
    inside = (global_rows >= 0) & (global_rows < total_rows)
    feat_rows = global_rows[1:-1]
    feat_inside = (feat_rows >= 0) & (feat_rows < total_rows)
    w_outputs = lax.dynamic_slice_in_dim(w_second, own_index * head_width, head_width, 1)
    w_taps = w_first.astype(jnp.float32)

    def features_of(ext):
        padded = jnp.pad(ext, ((0, 0), (0, 0), (2, 2))).astype(jnp.float32)
        maps = None
        tap_index = 0
        for shift_y in (-2, 0, 2):
            for shift_x in (-2, 0, 2):
                window = padded[:, 2 + shift_y : 2 + shift_y + first_rows, 2 + shift_x : 2 + shift_x + columns]
                term = w_taps[:, tap_index, None, None, None] * window[None]
                maps = term if maps is None else maps + term
                tap_index += 1
        maps = jnp.where(inside, jnp.maximum(maps, 0.0), 0.0).astype(jnp.bfloat16)
        mixed = second_terms(w_outputs, maps)
        return jnp.where(feat_inside, jnp.maximum(mixed, 0.0), 0.0).astype(jnp.bfloat16)

    framed = features_of(jnp.concatenate([prev_ext, own_ext], axis=0))

    current = framed[:, 1:, 4 : 4 + strip_rows, :]
    earlier = jnp.pad(framed[:, :sec_local], ((0, 0), (0, 0), (0, 0), (4, 4)))
    factor = score_scale / head_width
    field_shape = (sec_local, strip_rows, columns)
    running_max = jnp.full(field_shape, -1e30, jnp.float32)
    weight_sum = jnp.zeros(field_shape, jnp.float32)
    along_y = jnp.zeros(field_shape, jnp.float32)
    along_x = jnp.zeros(field_shape, jnp.float32)
    step_cols = lax.broadcasted_iota(jnp.float32, (9, 1, 1, 1), 0) - 4.0
    for shift_y in range(9):
        scores = (
            jnp.stack(
                [
                    jnp.einsum(
                        "cspw,cspw->spw",
                        current,
                        earlier[:, :, shift_y : shift_y + strip_rows, shift_x : shift_x + columns],
                        preferred_element_type=jnp.float32,
                    )
                    for shift_x in range(9)
                ]
            )
            * factor
        )
        highest = jnp.maximum(running_max, jnp.max(scores, axis=0))
        rescale = jnp.exp(running_max - highest)
        weights = jnp.exp(scores - highest)
        block_sum = jnp.sum(weights, axis=0)
        weight_sum = weight_sum * rescale + block_sum
        along_y = along_y * rescale + (shift_y - 4.0) * block_sum
        along_x = along_x * rescale + jnp.sum(weights * step_cols, axis=0)
        running_max = highest
    head_flow = jnp.stack([along_y / weight_sum, along_x / weight_sum], axis=1)

    sc = ("strip", "chan")
    sc_sizes = (n_strip, n_chan)
    flow_slots = [jnp.zeros_like(head_flow) for _ in range(n_strip)]
    for k in range(n_strip * n_chan):
        if k == 0:
            got = head_flow
        else:
            got = shifted_from(head_flow, sc, sc_sizes, (k // n_chan, k % n_chan), cyclic=True)
        src_strip = (strip_index - k // n_chan) % n_strip
        for slot in range(n_strip):
            flow_slots[slot] = flow_slots[slot] + jnp.where(src_strip == slot, got, 0.0)
    flows_full = jnp.concatenate(flow_slots, axis=2) / n_chan

    base_terms = flows_full + q_full.astype(jnp.float32) * 0.125
    split = n_chan == 2
    if split:
        base_terms = lax.dynamic_slice_in_dim(base_terms, own_index, 1, 1)
    comps = base_terms.shape[1]

    def chain_local(incoming):
        src = incoming
        outs = []
        for local_sec in range(sec_local):
            src = base_terms[local_sec] + sample(
                jnp.pad(src, ((0, 0), (4, 4), (4, 4))), q_full[local_sec], 4
            )
            outs.append(src)
        return outs

    warp_inputs = [framed[:, local_sec + 1] for local_sec in range(sec_local)]
    outs = chain_local(jnp.zeros((comps, total_rows, columns), jnp.float32))
    pending = list(range(sec_local))
    for turn in range(1, n_sec):
        carry = outs[-1]
        if pending:
            slot = pending.pop(0)
            carry, warp_inputs[slot] = lax.optimization_barrier((carry, warp_inputs[slot]))
        incoming = shifted_from(carry, ("sec",), (n_sec,), (1,))
        outs = chain_local(incoming)
    warped = jnp.stack(
        [
            sample(jnp.pad(warp_inputs[l], ((0, 0), (0, 0), (4, 4))), offsets[l], 4).astype(
                jnp.bfloat16
            )
            for l in range(sec_local)
        ]
    )
    composed = jnp.stack(
        [lax.dynamic_slice_in_dim(o, strip_first, strip_rows, 1) for o in outs]
    )
    if split:
        other = shifted_from(composed, ("chan",), (n_chan,), (1,), cyclic=True)
        composed = jnp.where(
            own_index == 0,
            jnp.concatenate([composed, other], axis=1),
            jnp.concatenate([other, composed], axis=1),
        )
    return (warped, composed)


def solution(mesh):
    in_specs = (
        P(("groups", "sec"), "strip", None),
        P(),
        P(),
        P(("groups", "sec"), None, "strip", None),
    )
    out_specs = (
        P(("groups", "sec"), "chan", "strip", None),
        P(("groups", "sec"), None, "strip", None),
    )
    return jax.shard_map(local, mesh=mesh, in_specs=in_specs, out_specs=out_specs, check_vma=False)
```

```python
import jax
import jax.numpy as jnp
from jax import lax
from jax.sharding import PartitionSpec as P

score_scale = 4.0


def shifted_from(value, axes, sizes, deltas, cyclic=False):
    pairs = []
    counts = [int(s) for s in sizes]
    total = 1
    for c in counts:
        total *= c
    for dst in range(total):
        coords = []
        rem = dst
        for c in reversed(counts):
            coords.append(rem % c)
            rem //= c
        coords = coords[::-1]
        src_coords = []
        ok = True
        for coord, c, d in zip(coords, counts, deltas):
            s = coord - d
            if cyclic:
                s %= c
            elif s < 0 or s >= c:
                ok = False
            src_coords.append(s)
        if not ok:
            continue
        src = 0
        for s, c in zip(src_coords, counts):
            src = src * c + s
        if src != dst:
            pairs.append((src, dst))
    if not pairs:
        return jnp.zeros_like(value)
    return lax.ppermute(value, axes if len(axes) > 1 else axes[0], pairs)


def first_taps(extended, rows_out, row_start):
    columns = extended.shape[-1]
    padded = jnp.pad(extended, ((0, 0), (0, 0), (2, 2)))
    tap_list = []
    for shift_y in (-2, 0, 2):
        for shift_x in (-2, 0, 2):
            tap_list.append(
                padded[
                    :,
                    row_start + shift_y : row_start + shift_y + rows_out,
                    2 + shift_x : 2 + shift_x + columns,
                ]
            )
    return jnp.stack(tap_list)


def second_terms(weights, inputs):
    rows_out = inputs.shape[2] - 2
    columns = inputs.shape[3]
    padded = jnp.pad(inputs, ((0, 0), (0, 0), (0, 0), (1, 1)))
    summed = None
    tap_index = 0
    for shift_y in (-1, 0, 1):
        for shift_x in (-1, 0, 1):
            window = padded[
                :, :, 1 + shift_y : 1 + shift_y + rows_out, 1 + shift_x : 1 + shift_x + columns
            ]
            tap_term = jnp.einsum(
                "oi,ispw->ospw", weights[tap_index], window, preferred_element_type=jnp.float32
            )
            summed = tap_term if summed is None else summed + tap_term
            tap_index += 1
    return summed


def hat_weights(quant_row):
    base = jnp.floor_divide(quant_row, 8)
    frac = (quant_row - 8 * base).astype(jnp.float32) * 0.125
    return [
        jnp.where(base == shift, 1.0 - frac, 0.0) + jnp.where(base + 1 == shift, frac, 0.0)
        for shift in range(-4, 5)
    ]


def sample(source, quant, row_start):
    rows_out, columns = (quant.shape[1], quant.shape[2])
    hats_y = hat_weights(quant[0])
    hats_x = hat_weights(quant[1])
    summed = jnp.zeros((source.shape[0], rows_out, columns), jnp.float32)
    for index_x in range(9):
        inner = jnp.zeros((source.shape[0], rows_out, columns), jnp.float32)
        for index_y in range(9):
            lower = row_start + index_y - 4
            window = source[:, lower : lower + rows_out, index_x : index_x + columns].astype(
                jnp.float32
            )
            inner = inner + hats_y[index_y] * window
        summed = summed + hats_x[index_x] * inner
    return summed


def local(sections, w_first, w_second, offsets):
    sec_local, strip_rows, columns = sections.shape
    n_sec = lax.axis_size("sec")
    n_strip = lax.axis_size("strip")
    n_chan = lax.axis_size("chan")
    strip_index = lax.axis_index("strip")
    own_index = lax.axis_index("chan")
    head_width = w_second.shape[1] // n_chan
    strip_first = strip_index * strip_rows
    total_rows = strip_rows * n_strip
    halo = 7
    ss = ("sec", "strip")
    ss_sizes = (n_sec, n_strip)

    if n_strip == 2:
        packed = jnp.concatenate(
            [sections[:, None].astype(jnp.float32), offsets.astype(jnp.float32)], axis=1
        ).astype(jnp.bfloat16)
        partner = shifted_from(packed, ("strip",), (n_strip,), (1,), cyclic=True)
        other_sec = partner[:, 0]
        from_left = jnp.where(strip_index == 1, other_sec[:, strip_rows - halo :], 0.0)
        from_right = jnp.where(strip_index == 0, other_sec[:, :halo], 0.0)
        other_q = partner[:, 1:].astype(jnp.int32)
        q_full = jnp.where(
            strip_index == 0,
            jnp.concatenate([offsets, other_q], axis=2),
            jnp.concatenate([other_q, offsets], axis=2),
        )
    else:
        from_left = shifted_from(sections[:, strip_rows - halo :], ("strip",), (n_strip,), (1,))
        from_right = shifted_from(sections[:, :halo], ("strip",), (n_strip,), (-1,))
        offset_parts = [offsets]
        for k in range(1, n_strip):
            offset_parts.append(shifted_from(offsets, ("strip",), (n_strip,), (k,), cyclic=True))
        offset_rows = []
        for slot in range(n_strip):
            piece = offset_parts[0]
            for k in range(1, n_strip):
                piece = jnp.where((strip_index - k) % n_strip == slot, offset_parts[k], piece)
            offset_rows.append(piece)
        q_full = jnp.concatenate(offset_rows, axis=2)
    own_ext = jnp.concatenate([from_left, sections, from_right], axis=1)
    prev_ext = shifted_from(own_ext[sec_local - 1 :], ("sec",), (n_sec,), (1,))

    first_rows = strip_rows + 10
    global_rows = strip_first - 5 + lax.broadcasted_iota(jnp.int32, (first_rows, 1), 0)
    inside = (global_rows >= 0) & (global_rows < total_rows)
    feat_rows = global_rows[1:-1]
    feat_inside = (feat_rows >= 0) & (feat_rows < total_rows)
    w_outputs = lax.dynamic_slice_in_dim(w_second, own_index * head_width, head_width, 1)
    w_taps = w_first.astype(jnp.float32)

    def features_of(ext):
        padded = jnp.pad(ext, ((0, 0), (0, 0), (2, 2))).astype(jnp.float32)
        maps = None
        tap_index = 0
        for shift_y in (-2, 0, 2):
            for shift_x in (-2, 0, 2):
                window = padded[:, 2 + shift_y : 2 + shift_y + first_rows, 2 + shift_x : 2 + shift_x + columns]
                term = w_taps[:, tap_index, None, None, None] * window[None]
                maps = term if maps is None else maps + term
                tap_index += 1
        maps = jnp.where(inside, jnp.maximum(maps, 0.0), 0.0).astype(jnp.bfloat16)
        mixed = second_terms(w_outputs, maps)
        return jnp.where(feat_inside, jnp.maximum(mixed, 0.0), 0.0).astype(jnp.bfloat16)

    framed = features_of(jnp.concatenate([prev_ext, own_ext], axis=0))

    current = framed[:, 1:, 4 : 4 + strip_rows, :]
    earlier = jnp.pad(framed[:, :sec_local], ((0, 0), (0, 0), (0, 0), (4, 4)))
    factor = score_scale / head_width
    field_shape = (sec_local, strip_rows, columns)
    running_max = jnp.full(field_shape, -1e30, jnp.float32)
    weight_sum = jnp.zeros(field_shape, jnp.float32)
    along_y = jnp.zeros(field_shape, jnp.float32)
    along_x = jnp.zeros(field_shape, jnp.float32)
    step_cols = lax.broadcasted_iota(jnp.float32, (9, 1, 1, 1), 0) - 4.0
    for shift_y in range(9):
        scores = (
            jnp.stack(
                [
                    jnp.einsum(
                        "cspw,cspw->spw",
                        current,
                        earlier[:, :, shift_y : shift_y + strip_rows, shift_x : shift_x + columns],
                        preferred_element_type=jnp.float32,
                    )
                    for shift_x in range(9)
                ]
            )
            * factor
        )
        highest = jnp.maximum(running_max, jnp.max(scores, axis=0))
        rescale = jnp.exp(running_max - highest)
        weights = jnp.exp(scores - highest)
        block_sum = jnp.sum(weights, axis=0)
        weight_sum = weight_sum * rescale + block_sum
        along_y = along_y * rescale + (shift_y - 4.0) * block_sum
        along_x = along_x * rescale + jnp.sum(weights * step_cols, axis=0)
        running_max = highest
    head_flow = jnp.stack([along_y / weight_sum, along_x / weight_sum], axis=1)

    pieces = [(0, 0, head_width)]
    chain_slots = max(n_sec - 1, 1)
    rest = sec_local - 1
    per_sec = max(1, -(-chain_slots // max(rest, 1))) if rest else 0
    for local_sec in range(1, sec_local):
        bounds = [round(head_width * k / per_sec) for k in range(per_sec + 1)]
        for lo_c, hi_c in zip(bounds[:-1], bounds[1:]):
            pieces.append((local_sec, lo_c, hi_c))
    warp_inputs = [framed[lo_c:hi_c, l + 1] for l, lo_c, hi_c in pieces]
    head_flow, warp_inputs[0] = lax.optimization_barrier((head_flow, warp_inputs[0]))

    sc = ("strip", "chan")
    sc_sizes = (n_strip, n_chan)
    flow_slots = [jnp.zeros_like(head_flow) for _ in range(n_strip)]
    for k in range(n_strip * n_chan):
        if k == 0:
            got = head_flow
        else:
            got = shifted_from(head_flow, sc, sc_sizes, (k // n_chan, k % n_chan), cyclic=True)
        src_strip = (strip_index - k // n_chan) % n_strip
        for slot in range(n_strip):
            flow_slots[slot] = flow_slots[slot] + jnp.where(src_strip == slot, got, 0.0)
    flows_full = jnp.concatenate(flow_slots, axis=2) / n_chan

    base_terms = flows_full + q_full.astype(jnp.float32) * 0.125
    split = n_chan == 2
    if split:
        base_terms = lax.dynamic_slice_in_dim(base_terms, own_index, 1, 1)
    comps = base_terms.shape[1]

    def chain_local(incoming):
        src = incoming
        outs = []
        for local_sec in range(sec_local):
            src = base_terms[local_sec] + sample(
                jnp.pad(src, ((0, 0), (4, 4), (4, 4))), q_full[local_sec], 4
            )
            outs.append(src)
        return outs

    outs = chain_local(jnp.zeros((comps, total_rows, columns), jnp.float32))
    pending = list(range(1, len(pieces)))
    for turn in range(1, n_sec):
        carry = outs[-1]
        if pending:
            slot = pending.pop(0)
            carry, warp_inputs[slot] = lax.optimization_barrier((carry, warp_inputs[slot]))
        incoming = shifted_from(carry, ("sec",), (n_sec,), (1,))
        outs = chain_local(incoming)
    warped_pieces = [
        sample(jnp.pad(src, ((0, 0), (0, 0), (4, 4))), offsets[l], 4).astype(jnp.bfloat16)
        for src, (l, _, _) in zip(warp_inputs, pieces)
    ]
    warped = jnp.stack(
        [
            jnp.concatenate([w for w, p in zip(warped_pieces, pieces) if p[0] == l], axis=0)
            for l in range(sec_local)
        ]
    )
    composed = jnp.stack(
        [lax.dynamic_slice_in_dim(o, strip_first, strip_rows, 1) for o in outs]
    )
    if split:
        other = shifted_from(composed, ("chan",), (n_chan,), (1,), cyclic=True)
        composed = jnp.where(
            own_index == 0,
            jnp.concatenate([composed, other], axis=1),
            jnp.concatenate([other, composed], axis=1),
        )
    return (warped, composed)


def solution(mesh):
    in_specs = (
        P(("groups", "sec"), "strip", None),
        P(),
        P(),
        P(("groups", "sec"), None, "strip", None),
    )
    out_specs = (
        P(("groups", "sec"), "chan", "strip", None),
        P(("groups", "sec"), None, "strip", None),
    )
    return jax.shard_map(local, mesh=mesh, in_specs=in_specs, out_specs=out_specs, check_vma=False)
```

```python
import jax
import jax.numpy as jnp
from jax import lax
from jax.sharding import PartitionSpec as P

score_scale = 4.0


def shifted_from(value, axes, sizes, deltas, cyclic=False):
    pairs = []
    counts = [int(s) for s in sizes]
    total = 1
    for c in counts:
        total *= c
    for dst in range(total):
        coords = []
        rem = dst
        for c in reversed(counts):
            coords.append(rem % c)
            rem //= c
        coords = coords[::-1]
        src_coords = []
        ok = True
        for coord, c, d in zip(coords, counts, deltas):
            s = coord - d
            if cyclic:
                s %= c
            elif s < 0 or s >= c:
                ok = False
            src_coords.append(s)
        if not ok:
            continue
        src = 0
        for s, c in zip(src_coords, counts):
            src = src * c + s
        if src != dst:
            pairs.append((src, dst))
    if not pairs:
        return jnp.zeros_like(value)
    return lax.ppermute(value, axes if len(axes) > 1 else axes[0], pairs)


def first_taps(extended, rows_out, row_start):
    columns = extended.shape[-1]
    padded = jnp.pad(extended, ((0, 0), (0, 0), (2, 2)))
    tap_list = []
    for shift_y in (-2, 0, 2):
        for shift_x in (-2, 0, 2):
            tap_list.append(
                padded[
                    :,
                    row_start + shift_y : row_start + shift_y + rows_out,
                    2 + shift_x : 2 + shift_x + columns,
                ]
            )
    return jnp.stack(tap_list)


def second_terms(weights, inputs):
    rows_out = inputs.shape[2] - 2
    columns = inputs.shape[3]
    padded = jnp.pad(inputs, ((0, 0), (0, 0), (0, 0), (1, 1)))
    summed = None
    tap_index = 0
    for shift_y in (-1, 0, 1):
        for shift_x in (-1, 0, 1):
            window = padded[
                :, :, 1 + shift_y : 1 + shift_y + rows_out, 1 + shift_x : 1 + shift_x + columns
            ]
            tap_term = jnp.einsum(
                "oi,ispw->ospw", weights[tap_index], window, preferred_element_type=jnp.float32
            )
            summed = tap_term if summed is None else summed + tap_term
            tap_index += 1
    return summed


def hat_weights(quant_row):
    base = jnp.floor_divide(quant_row, 8)
    frac = (quant_row - 8 * base).astype(jnp.float32) * 0.125
    return [
        jnp.where(base == shift, 1.0 - frac, 0.0) + jnp.where(base + 1 == shift, frac, 0.0)
        for shift in range(-4, 5)
    ]


def sample(source, quant, row_start):
    rows_out, columns = (quant.shape[1], quant.shape[2])
    hats_y = hat_weights(quant[0])
    hats_x = hat_weights(quant[1])
    summed = jnp.zeros((source.shape[0], rows_out, columns), jnp.float32)
    for index_x in range(9):
        inner = jnp.zeros((source.shape[0], rows_out, columns), jnp.float32)
        for index_y in range(9):
            lower = row_start + index_y - 4
            window = source[:, lower : lower + rows_out, index_x : index_x + columns].astype(
                jnp.float32
            )
            inner = inner + hats_y[index_y] * window
        summed = summed + hats_x[index_x] * inner
    return summed


def local(sections, w_first, w_second, offsets):
    sec_local, strip_rows, columns = sections.shape
    n_sec = lax.axis_size("sec")
    n_strip = lax.axis_size("strip")
    n_chan = lax.axis_size("chan")
    strip_index = lax.axis_index("strip")
    own_index = lax.axis_index("chan")
    head_width = w_second.shape[1] // n_chan
    strip_first = strip_index * strip_rows
    total_rows = strip_rows * n_strip
    halo = 7
    ss = ("sec", "strip")
    ss_sizes = (n_sec, n_strip)

    if n_strip == 2:
        packed = jnp.concatenate(
            [sections[:, None].astype(jnp.float32), offsets.astype(jnp.float32)], axis=1
        ).astype(jnp.bfloat16)
        partner = shifted_from(packed, ("strip",), (n_strip,), (1,), cyclic=True)
        other_sec = partner[:, 0]
        from_left = jnp.where(strip_index == 1, other_sec[:, strip_rows - halo :], 0.0)
        from_right = jnp.where(strip_index == 0, other_sec[:, :halo], 0.0)
        other_q = partner[:, 1:].astype(jnp.int32)
        q_full = jnp.where(
            strip_index == 0,
            jnp.concatenate([offsets, other_q], axis=2),
            jnp.concatenate([other_q, offsets], axis=2),
        )
    else:
        from_left = shifted_from(sections[:, strip_rows - halo :], ("strip",), (n_strip,), (1,))
        from_right = shifted_from(sections[:, :halo], ("strip",), (n_strip,), (-1,))
        offset_parts = [offsets]
        for k in range(1, n_strip):
            offset_parts.append(shifted_from(offsets, ("strip",), (n_strip,), (k,), cyclic=True))
        offset_rows = []
        for slot in range(n_strip):
            piece = offset_parts[0]
            for k in range(1, n_strip):
                piece = jnp.where((strip_index - k) % n_strip == slot, offset_parts[k], piece)
            offset_rows.append(piece)
        q_full = jnp.concatenate(offset_rows, axis=2)
    own_ext = jnp.concatenate([from_left, sections, from_right], axis=1)
    prev_ext = shifted_from(own_ext[sec_local - 1 :], ("sec",), (n_sec,), (1,))

    first_rows = strip_rows + 10
    global_rows = strip_first - 5 + lax.broadcasted_iota(jnp.int32, (first_rows, 1), 0)
    inside = (global_rows >= 0) & (global_rows < total_rows)
    feat_rows = global_rows[1:-1]
    feat_inside = (feat_rows >= 0) & (feat_rows < total_rows)
    w_outputs = lax.dynamic_slice_in_dim(w_second, own_index * head_width, head_width, 1)
    w_taps = w_first.astype(jnp.float32)

    def features_of(ext):
        padded = jnp.pad(ext, ((0, 0), (0, 0), (2, 2))).astype(jnp.float32)
        maps = None
        tap_index = 0
        for shift_y in (-2, 0, 2):
            for shift_x in (-2, 0, 2):
                window = padded[:, 2 + shift_y : 2 + shift_y + first_rows, 2 + shift_x : 2 + shift_x + columns]
                term = w_taps[:, tap_index, None, None, None] * window[None]
                maps = term if maps is None else maps + term
                tap_index += 1
        maps = jnp.where(inside, jnp.maximum(maps, 0.0), 0.0).astype(jnp.bfloat16)
        mixed = second_terms(w_outputs, maps)
        return jnp.where(feat_inside, jnp.maximum(mixed, 0.0), 0.0).astype(jnp.bfloat16)

    framed = features_of(jnp.concatenate([prev_ext, own_ext], axis=0))

    current = framed[:, 1:, 4 : 4 + strip_rows, :]
    earlier = jnp.pad(framed[:, :sec_local], ((0, 0), (0, 0), (0, 0), (4, 4)))
    factor = score_scale / head_width
    field_shape = (sec_local, strip_rows, columns)
    running_max = jnp.full(field_shape, -1e30, jnp.float32)
    weight_sum = jnp.zeros(field_shape, jnp.float32)
    along_y = jnp.zeros(field_shape, jnp.float32)
    along_x = jnp.zeros(field_shape, jnp.float32)
    step_cols = lax.broadcasted_iota(jnp.float32, (9, 1, 1, 1), 0) - 4.0
    def corr_block(shift_y, state):
        running_max, weight_sum, along_y, along_x = state
        rows = lax.dynamic_slice_in_dim(earlier, shift_y, strip_rows, 2)
        scores = (
            jnp.stack(
                [
                    jnp.einsum(
                        "cspw,cspw->spw",
                        current,
                        rows[:, :, :, shift_x : shift_x + columns],
                        preferred_element_type=jnp.float32,
                    )
                    for shift_x in range(9)
                ]
            )
            * factor
        )
        highest = jnp.maximum(running_max, jnp.max(scores, axis=0))
        rescale = jnp.exp(running_max - highest)
        weights = jnp.exp(scores - highest)
        block_sum = jnp.sum(weights, axis=0)
        weight_sum = weight_sum * rescale + block_sum
        along_y = along_y * rescale + (shift_y.astype(jnp.float32) - 4.0) * block_sum
        along_x = along_x * rescale + jnp.sum(weights * step_cols, axis=0)
        return (highest, weight_sum, along_y, along_x)

    running_max, weight_sum, along_y, along_x = lax.fori_loop(
        0, 9, corr_block, (running_max, weight_sum, along_y, along_x)
    )
    head_flow = jnp.stack([along_y / weight_sum, along_x / weight_sum], axis=1)

    pieces = [(0, 0, head_width)]
    chain_slots = max(n_sec - 1, 1)
    rest = sec_local - 1
    per_sec = max(1, -(-chain_slots // max(rest, 1))) if rest else 0
    for local_sec in range(1, sec_local):
        bounds = [round(head_width * k / per_sec) for k in range(per_sec + 1)]
        for lo_c, hi_c in zip(bounds[:-1], bounds[1:]):
            pieces.append((local_sec, lo_c, hi_c))
    warp_inputs = [framed[lo_c:hi_c, l + 1] for l, lo_c, hi_c in pieces]
    head_flow, warp_inputs[0] = lax.optimization_barrier((head_flow, warp_inputs[0]))

    sc = ("strip", "chan")
    sc_sizes = (n_strip, n_chan)
    flow_slots = [jnp.zeros_like(head_flow) for _ in range(n_strip)]
    for k in range(n_strip * n_chan):
        if k == 0:
            got = head_flow
        else:
            got = shifted_from(head_flow, sc, sc_sizes, (k // n_chan, k % n_chan), cyclic=True)
        src_strip = (strip_index - k // n_chan) % n_strip
        for slot in range(n_strip):
            flow_slots[slot] = flow_slots[slot] + jnp.where(src_strip == slot, got, 0.0)
    flows_full = jnp.concatenate(flow_slots, axis=2) / n_chan

    base_terms = flows_full + q_full.astype(jnp.float32) * 0.125
    split = n_chan == 2
    if split:
        base_terms = lax.dynamic_slice_in_dim(base_terms, own_index, 1, 1)
    comps = base_terms.shape[1]

    def chain_local(incoming):
        src = incoming
        outs = []
        for local_sec in range(sec_local):
            src = base_terms[local_sec] + sample(
                jnp.pad(src, ((0, 0), (4, 4), (4, 4))), q_full[local_sec], 4
            )
            outs.append(src)
        return outs

    outs = chain_local(jnp.zeros((comps, total_rows, columns), jnp.float32))
    pending = list(range(1, len(pieces)))
    for turn in range(1, n_sec):
        carry = outs[-1]
        if pending:
            slot = pending.pop(0)
            carry, warp_inputs[slot] = lax.optimization_barrier((carry, warp_inputs[slot]))
        incoming = shifted_from(carry, ("sec",), (n_sec,), (1,))
        outs = chain_local(incoming)
    warped_pieces = [
        sample(jnp.pad(src, ((0, 0), (0, 0), (4, 4))), offsets[l], 4).astype(jnp.bfloat16)
        for src, (l, _, _) in zip(warp_inputs, pieces)
    ]
    warped = jnp.stack(
        [
            jnp.concatenate([w for w, p in zip(warped_pieces, pieces) if p[0] == l], axis=0)
            for l in range(sec_local)
        ]
    )
    composed = jnp.stack(
        [lax.dynamic_slice_in_dim(o, strip_first, strip_rows, 1) for o in outs]
    )
    if split:
        other = shifted_from(composed, ("chan",), (n_chan,), (1,), cyclic=True)
        composed = jnp.where(
            own_index == 0,
            jnp.concatenate([composed, other], axis=1),
            jnp.concatenate([other, composed], axis=1),
        )
    return (warped, composed)


def solution(mesh):
    in_specs = (
        P(("groups", "sec"), "strip", None),
        P(),
        P(),
        P(("groups", "sec"), None, "strip", None),
    )
    out_specs = (
        P(("groups", "sec"), "chan", "strip", None),
        P(("groups", "sec"), None, "strip", None),
    )
    return jax.shard_map(local, mesh=mesh, in_specs=in_specs, out_specs=out_specs, check_vma=False)
```

```python
import jax
import jax.numpy as jnp
from jax import lax
from jax.sharding import PartitionSpec as P

score_scale = 4.0


def shifted_from(value, axes, sizes, deltas, cyclic=False):
    pairs = []
    counts = [int(s) for s in sizes]
    total = 1
    for c in counts:
        total *= c
    for dst in range(total):
        coords = []
        rem = dst
        for c in reversed(counts):
            coords.append(rem % c)
            rem //= c
        coords = coords[::-1]
        src_coords = []
        ok = True
        for coord, c, d in zip(coords, counts, deltas):
            s = coord - d
            if cyclic:
                s %= c
            elif s < 0 or s >= c:
                ok = False
            src_coords.append(s)
        if not ok:
            continue
        src = 0
        for s, c in zip(src_coords, counts):
            src = src * c + s
        if src != dst:
            pairs.append((src, dst))
    if not pairs:
        return jnp.zeros_like(value)
    return lax.ppermute(value, axes if len(axes) > 1 else axes[0], pairs)


def first_taps(extended, rows_out, row_start):
    columns = extended.shape[-1]
    padded = jnp.pad(extended, ((0, 0), (0, 0), (2, 2)))
    tap_list = []
    for shift_y in (-2, 0, 2):
        for shift_x in (-2, 0, 2):
            tap_list.append(
                padded[
                    :,
                    row_start + shift_y : row_start + shift_y + rows_out,
                    2 + shift_x : 2 + shift_x + columns,
                ]
            )
    return jnp.stack(tap_list)


def second_terms(weights, inputs):
    rows_out = inputs.shape[2] - 2
    columns = inputs.shape[3]
    padded = jnp.pad(inputs, ((0, 0), (0, 0), (0, 0), (1, 1)))
    summed = None
    tap_index = 0
    for shift_y in (-1, 0, 1):
        for shift_x in (-1, 0, 1):
            window = padded[
                :, :, 1 + shift_y : 1 + shift_y + rows_out, 1 + shift_x : 1 + shift_x + columns
            ]
            tap_term = jnp.einsum(
                "oi,ispw->ospw", weights[tap_index], window, preferred_element_type=jnp.float32
            )
            summed = tap_term if summed is None else summed + tap_term
            tap_index += 1
    return summed


def hat_weights(quant_row):
    base = jnp.floor_divide(quant_row, 8)
    frac = (quant_row - 8 * base).astype(jnp.float32) * 0.125
    return [
        jnp.where(base == shift, 1.0 - frac, 0.0) + jnp.where(base + 1 == shift, frac, 0.0)
        for shift in range(-4, 5)
    ]


def sample(source, quant, row_start):
    rows_out, columns = (quant.shape[1], quant.shape[2])
    hats_y = hat_weights(quant[0])
    hats_x = hat_weights(quant[1])
    summed = jnp.zeros((source.shape[0], rows_out, columns), jnp.float32)
    for index_x in range(9):
        inner = jnp.zeros((source.shape[0], rows_out, columns), jnp.float32)
        for index_y in range(9):
            lower = row_start + index_y - 4
            window = source[:, lower : lower + rows_out, index_x : index_x + columns].astype(
                jnp.float32
            )
            inner = inner + hats_y[index_y] * window
        summed = summed + hats_x[index_x] * inner
    return summed


def local(sections, w_first, w_second, offsets):
    sec_local, strip_rows, columns = sections.shape
    n_sec = lax.axis_size("sec")
    n_strip = lax.axis_size("strip")
    n_chan = lax.axis_size("chan")
    strip_index = lax.axis_index("strip")
    own_index = lax.axis_index("chan")
    head_width = w_second.shape[1] // n_chan
    strip_first = strip_index * strip_rows
    total_rows = strip_rows * n_strip
    halo = 7
    ss = ("sec", "strip")
    ss_sizes = (n_sec, n_strip)

    if n_strip == 2:
        packed = jnp.concatenate(
            [sections[:, None].astype(jnp.float32), offsets.astype(jnp.float32)], axis=1
        ).astype(jnp.bfloat16)
        partner = shifted_from(packed, ("strip",), (n_strip,), (1,), cyclic=True)
        other_sec = partner[:, 0]
        from_left = jnp.where(strip_index == 1, other_sec[:, strip_rows - halo :], 0.0)
        from_right = jnp.where(strip_index == 0, other_sec[:, :halo], 0.0)
        other_q = partner[:, 1:].astype(jnp.int32)
        q_full = jnp.where(
            strip_index == 0,
            jnp.concatenate([offsets, other_q], axis=2),
            jnp.concatenate([other_q, offsets], axis=2),
        )
    else:
        from_left = shifted_from(sections[:, strip_rows - halo :], ("strip",), (n_strip,), (1,))
        from_right = shifted_from(sections[:, :halo], ("strip",), (n_strip,), (-1,))
        offset_parts = [offsets]
        for k in range(1, n_strip):
            offset_parts.append(shifted_from(offsets, ("strip",), (n_strip,), (k,), cyclic=True))
        offset_rows = []
        for slot in range(n_strip):
            piece = offset_parts[0]
            for k in range(1, n_strip):
                piece = jnp.where((strip_index - k) % n_strip == slot, offset_parts[k], piece)
            offset_rows.append(piece)
        q_full = jnp.concatenate(offset_rows, axis=2)
    own_ext = jnp.concatenate([from_left, sections, from_right], axis=1)
    prev_ext = shifted_from(own_ext[sec_local - 1 :], ("sec",), (n_sec,), (1,))

    first_rows = strip_rows + 10
    global_rows = strip_first - 5 + lax.broadcasted_iota(jnp.int32, (first_rows, 1), 0)
    inside = (global_rows >= 0) & (global_rows < total_rows)
    feat_rows = global_rows[1:-1]
    feat_inside = (feat_rows >= 0) & (feat_rows < total_rows)
    w_outputs = lax.dynamic_slice_in_dim(w_second, own_index * head_width, head_width, 1)
    w_taps = w_first.astype(jnp.float32)

    def features_of(ext):
        padded = jnp.pad(ext, ((0, 0), (0, 0), (2, 2))).astype(jnp.float32)
        maps = None
        tap_index = 0
        for shift_y in (-2, 0, 2):
            for shift_x in (-2, 0, 2):
                window = padded[:, 2 + shift_y : 2 + shift_y + first_rows, 2 + shift_x : 2 + shift_x + columns]
                term = w_taps[:, tap_index, None, None, None] * window[None]
                maps = term if maps is None else maps + term
                tap_index += 1
        maps = jnp.where(inside, jnp.maximum(maps, 0.0), 0.0).astype(jnp.bfloat16)
        mixed = second_terms(w_outputs, maps)
        return jnp.where(feat_inside, jnp.maximum(mixed, 0.0), 0.0).astype(jnp.bfloat16)

    framed = features_of(jnp.concatenate([prev_ext, own_ext], axis=0))

    current = framed[:, 1:, 4 : 4 + strip_rows, :].astype(jnp.float32)
    earlier = jnp.pad(framed[:, :sec_local], ((0, 0), (0, 0), (0, 0), (4, 4))).astype(jnp.float32)
    factor = score_scale / head_width
    field_shape = (sec_local, strip_rows, columns)
    running_max = jnp.full(field_shape, -1e30, jnp.float32)
    weight_sum = jnp.zeros(field_shape, jnp.float32)
    along_y = jnp.zeros(field_shape, jnp.float32)
    along_x = jnp.zeros(field_shape, jnp.float32)
    step_cols = lax.broadcasted_iota(jnp.float32, (9, 1, 1, 1), 0) - 4.0
    for shift_y in range(9):
        scores = (
            jnp.stack(
                [
                    jnp.einsum(
                        "cspw,cspw->spw",
                        current,
                        earlier[:, :, shift_y : shift_y + strip_rows, shift_x : shift_x + columns],
                        preferred_element_type=jnp.float32,
                    )
                    for shift_x in range(9)
                ]
            )
            * factor
        )
        highest = jnp.maximum(running_max, jnp.max(scores, axis=0))
        rescale = jnp.exp(running_max - highest)
        weights = jnp.exp(scores - highest)
        block_sum = jnp.sum(weights, axis=0)
        weight_sum = weight_sum * rescale + block_sum
        along_y = along_y * rescale + (shift_y - 4.0) * block_sum
        along_x = along_x * rescale + jnp.sum(weights * step_cols, axis=0)
        running_max = highest
    head_flow = jnp.stack([along_y / weight_sum, along_x / weight_sum], axis=1)

    pieces = [(0, 0, head_width)]
    chain_slots = max(n_sec - 1, 1)
    rest = sec_local - 1
    per_sec = max(1, -(-chain_slots // max(rest, 1))) if rest else 0
    for local_sec in range(1, sec_local):
        bounds = [round(head_width * k / per_sec) for k in range(per_sec + 1)]
        for lo_c, hi_c in zip(bounds[:-1], bounds[1:]):
            pieces.append((local_sec, lo_c, hi_c))
    warp_inputs = [framed[lo_c:hi_c, l + 1] for l, lo_c, hi_c in pieces]
    head_flow, warp_inputs[0] = lax.optimization_barrier((head_flow, warp_inputs[0]))

    sc = ("strip", "chan")
    sc_sizes = (n_strip, n_chan)
    flow_slots = [jnp.zeros_like(head_flow) for _ in range(n_strip)]
    for k in range(n_strip * n_chan):
        if k == 0:
            got = head_flow
        else:
            got = shifted_from(head_flow, sc, sc_sizes, (k // n_chan, k % n_chan), cyclic=True)
        src_strip = (strip_index - k // n_chan) % n_strip
        for slot in range(n_strip):
            flow_slots[slot] = flow_slots[slot] + jnp.where(src_strip == slot, got, 0.0)
    flows_full = jnp.concatenate(flow_slots, axis=2) / n_chan

    base_terms = flows_full + q_full.astype(jnp.float32) * 0.125
    split = n_chan == 2
    if split:
        base_terms = lax.dynamic_slice_in_dim(base_terms, own_index, 1, 1)
    comps = base_terms.shape[1]

    def chain_local(incoming):
        src = incoming
        outs = []
        for local_sec in range(sec_local):
            src = base_terms[local_sec] + sample(
                jnp.pad(src, ((0, 0), (4, 4), (4, 4))), q_full[local_sec], 4
            )
            outs.append(src)
        return outs

    outs = chain_local(jnp.zeros((comps, total_rows, columns), jnp.float32))
    pending = list(range(1, len(pieces)))
    for turn in range(1, n_sec):
        carry = outs[-1]
        if pending:
            slot = pending.pop(0)
            carry, warp_inputs[slot] = lax.optimization_barrier((carry, warp_inputs[slot]))
        incoming = shifted_from(carry, ("sec",), (n_sec,), (1,))
        outs = chain_local(incoming)
    warped_pieces = [
        sample(jnp.pad(src.astype(jnp.float32), ((0, 0), (0, 0), (4, 4))), offsets[l], 4).astype(
            jnp.bfloat16
        )
        for src, (l, _, _) in zip(warp_inputs, pieces)
    ]
    warped = jnp.stack(
        [
            jnp.concatenate([w for w, p in zip(warped_pieces, pieces) if p[0] == l], axis=0)
            for l in range(sec_local)
        ]
    )
    composed = jnp.stack(
        [lax.dynamic_slice_in_dim(o, strip_first, strip_rows, 1) for o in outs]
    )
    if split:
        other = shifted_from(composed, ("chan",), (n_chan,), (1,), cyclic=True)
        composed = jnp.where(
            own_index == 0,
            jnp.concatenate([composed, other], axis=1),
            jnp.concatenate([other, composed], axis=1),
        )
    return (warped, composed)


def solution(mesh):
    in_specs = (
        P(("groups", "sec"), "strip", None),
        P(),
        P(),
        P(("groups", "sec"), None, "strip", None),
    )
    out_specs = (
        P(("groups", "sec"), "chan", "strip", None),
        P(("groups", "sec"), None, "strip", None),
    )
    return jax.shard_map(local, mesh=mesh, in_specs=in_specs, out_specs=out_specs, check_vma=False)
```

```python
import jax
import jax.numpy as jnp
from jax import lax
from jax.sharding import PartitionSpec as P

score_scale = 4.0


def shifted_from(value, axes, sizes, deltas, cyclic=False):
    pairs = []
    counts = [int(s) for s in sizes]
    total = 1
    for c in counts:
        total *= c
    for dst in range(total):
        coords = []
        rem = dst
        for c in reversed(counts):
            coords.append(rem % c)
            rem //= c
        coords = coords[::-1]
        src_coords = []
        ok = True
        for coord, c, d in zip(coords, counts, deltas):
            s = coord - d
            if cyclic:
                s %= c
            elif s < 0 or s >= c:
                ok = False
            src_coords.append(s)
        if not ok:
            continue
        src = 0
        for s, c in zip(src_coords, counts):
            src = src * c + s
        if src != dst:
            pairs.append((src, dst))
    if not pairs:
        return jnp.zeros_like(value)
    return lax.ppermute(value, axes if len(axes) > 1 else axes[0], pairs)


def first_taps(extended, rows_out, row_start):
    columns = extended.shape[-1]
    padded = jnp.pad(extended, ((0, 0), (0, 0), (2, 2)))
    tap_list = []
    for shift_y in (-2, 0, 2):
        for shift_x in (-2, 0, 2):
            tap_list.append(
                padded[
                    :,
                    row_start + shift_y : row_start + shift_y + rows_out,
                    2 + shift_x : 2 + shift_x + columns,
                ]
            )
    return jnp.stack(tap_list)


def second_terms(weights, inputs):
    rows_out = inputs.shape[2] - 2
    columns = inputs.shape[3]
    left = jnp.pad(inputs, ((0, 0), (0, 0), (0, 0), (1, 0)))[..., :columns]
    right = jnp.pad(inputs, ((0, 0), (0, 0), (0, 0), (0, 1)))[..., 1:]
    left, right = lax.optimization_barrier((left, right))
    by_shift = {-1: left, 0: inputs, 1: right}
    summed = None
    tap_index = 0
    for shift_y in (-1, 0, 1):
        for shift_x in (-1, 0, 1):
            window = by_shift[shift_x][:, :, 1 + shift_y : 1 + shift_y + rows_out, :]
            tap_term = jnp.einsum(
                "oi,ispw->ospw", weights[tap_index], window, preferred_element_type=jnp.float32
            )
            summed = tap_term if summed is None else summed + tap_term
            tap_index += 1
    return summed


def hat_weights(quant_row):
    base = jnp.floor_divide(quant_row, 8)
    frac = (quant_row - 8 * base).astype(jnp.float32) * 0.125
    return [
        jnp.where(base == shift, 1.0 - frac, 0.0) + jnp.where(base + 1 == shift, frac, 0.0)
        for shift in range(-4, 5)
    ]


def sample(source, quant, row_start):
    rows_out, columns = (quant.shape[1], quant.shape[2])
    hats_y = hat_weights(quant[0])
    hats_x = hat_weights(quant[1])
    summed = jnp.zeros((source.shape[0], rows_out, columns), jnp.float32)
    for index_x in range(9):
        inner = jnp.zeros((source.shape[0], rows_out, columns), jnp.float32)
        for index_y in range(9):
            lower = row_start + index_y - 4
            window = source[:, lower : lower + rows_out, index_x : index_x + columns].astype(
                jnp.float32
            )
            inner = inner + hats_y[index_y] * window
        summed = summed + hats_x[index_x] * inner
    return summed


def local(sections, w_first, w_second, offsets):
    sec_local, strip_rows, columns = sections.shape
    n_sec = lax.axis_size("sec")
    n_strip = lax.axis_size("strip")
    n_chan = lax.axis_size("chan")
    strip_index = lax.axis_index("strip")
    own_index = lax.axis_index("chan")
    head_width = w_second.shape[1] // n_chan
    strip_first = strip_index * strip_rows
    total_rows = strip_rows * n_strip
    halo = 7
    ss = ("sec", "strip")
    ss_sizes = (n_sec, n_strip)

    if n_strip == 2:
        packed = jnp.concatenate(
            [sections[:, None].astype(jnp.float32), offsets.astype(jnp.float32)], axis=1
        ).astype(jnp.bfloat16)
        partner = shifted_from(packed, ("strip",), (n_strip,), (1,), cyclic=True)
        other_sec = partner[:, 0]
        from_left = jnp.where(strip_index == 1, other_sec[:, strip_rows - halo :], 0.0)
        from_right = jnp.where(strip_index == 0, other_sec[:, :halo], 0.0)
        other_q = partner[:, 1:].astype(jnp.int32)
        q_full = jnp.where(
            strip_index == 0,
            jnp.concatenate([offsets, other_q], axis=2),
            jnp.concatenate([other_q, offsets], axis=2),
        )
    else:
        from_left = shifted_from(sections[:, strip_rows - halo :], ("strip",), (n_strip,), (1,))
        from_right = shifted_from(sections[:, :halo], ("strip",), (n_strip,), (-1,))
        offset_parts = [offsets]
        for k in range(1, n_strip):
            offset_parts.append(shifted_from(offsets, ("strip",), (n_strip,), (k,), cyclic=True))
        offset_rows = []
        for slot in range(n_strip):
            piece = offset_parts[0]
            for k in range(1, n_strip):
                piece = jnp.where((strip_index - k) % n_strip == slot, offset_parts[k], piece)
            offset_rows.append(piece)
        q_full = jnp.concatenate(offset_rows, axis=2)
    own_ext = jnp.concatenate([from_left, sections, from_right], axis=1)
    prev_ext = shifted_from(own_ext[sec_local - 1 :], ("sec",), (n_sec,), (1,))

    first_rows = strip_rows + 10
    global_rows = strip_first - 5 + lax.broadcasted_iota(jnp.int32, (first_rows, 1), 0)
    inside = (global_rows >= 0) & (global_rows < total_rows)
    feat_rows = global_rows[1:-1]
    feat_inside = (feat_rows >= 0) & (feat_rows < total_rows)
    w_outputs = lax.dynamic_slice_in_dim(w_second, own_index * head_width, head_width, 1)
    w_taps = w_first.astype(jnp.float32)

    def features_of(ext):
        padded = jnp.pad(ext, ((0, 0), (0, 0), (2, 2))).astype(jnp.float32)
        maps = None
        tap_index = 0
        for shift_y in (-2, 0, 2):
            for shift_x in (-2, 0, 2):
                window = padded[:, 2 + shift_y : 2 + shift_y + first_rows, 2 + shift_x : 2 + shift_x + columns]
                term = w_taps[:, tap_index, None, None, None] * window[None]
                maps = term if maps is None else maps + term
                tap_index += 1
        maps = jnp.where(inside, jnp.maximum(maps, 0.0), 0.0).astype(jnp.bfloat16)
        mixed = second_terms(w_outputs, maps)
        return jnp.where(feat_inside, jnp.maximum(mixed, 0.0), 0.0).astype(jnp.bfloat16)

    framed = features_of(jnp.concatenate([prev_ext, own_ext], axis=0))

    current = framed[:, 1:, 4 : 4 + strip_rows, :]
    earlier = jnp.pad(framed[:, :sec_local], ((0, 0), (0, 0), (0, 0), (4, 4)))
    factor = score_scale / head_width
    field_shape = (sec_local, strip_rows, columns)
    running_max = jnp.full(field_shape, -1e30, jnp.float32)
    weight_sum = jnp.zeros(field_shape, jnp.float32)
    along_y = jnp.zeros(field_shape, jnp.float32)
    along_x = jnp.zeros(field_shape, jnp.float32)
    step_cols = lax.broadcasted_iota(jnp.float32, (9, 1, 1, 1), 0) - 4.0
    for shift_y in range(9):
        scores = (
            jnp.stack(
                [
                    jnp.einsum(
                        "cspw,cspw->spw",
                        current,
                        earlier[:, :, shift_y : shift_y + strip_rows, shift_x : shift_x + columns],
                        preferred_element_type=jnp.float32,
                    )
                    for shift_x in range(9)
                ]
            )
            * factor
        )
        highest = jnp.maximum(running_max, jnp.max(scores, axis=0))
        rescale = jnp.exp(running_max - highest)
        weights = jnp.exp(scores - highest)
        block_sum = jnp.sum(weights, axis=0)
        weight_sum = weight_sum * rescale + block_sum
        along_y = along_y * rescale + (shift_y - 4.0) * block_sum
        along_x = along_x * rescale + jnp.sum(weights * step_cols, axis=0)
        running_max = highest
    head_flow = jnp.stack([along_y / weight_sum, along_x / weight_sum], axis=1)

    pieces = [(0, 0, head_width)]
    chain_slots = max(n_sec - 1, 1)
    rest = sec_local - 1
    per_sec = max(1, -(-chain_slots // max(rest, 1))) if rest else 0
    for local_sec in range(1, sec_local):
        bounds = [round(head_width * k / per_sec) for k in range(per_sec + 1)]
        for lo_c, hi_c in zip(bounds[:-1], bounds[1:]):
            pieces.append((local_sec, lo_c, hi_c))
    warp_inputs = [framed[lo_c:hi_c, l + 1] for l, lo_c, hi_c in pieces]
    head_flow, warp_inputs[0] = lax.optimization_barrier((head_flow, warp_inputs[0]))

    sc = ("strip", "chan")
    sc_sizes = (n_strip, n_chan)
    flow_slots = [jnp.zeros_like(head_flow) for _ in range(n_strip)]
    for k in range(n_strip * n_chan):
        if k == 0:
            got = head_flow
        else:
            got = shifted_from(head_flow, sc, sc_sizes, (k // n_chan, k % n_chan), cyclic=True)
        src_strip = (strip_index - k // n_chan) % n_strip
        for slot in range(n_strip):
            flow_slots[slot] = flow_slots[slot] + jnp.where(src_strip == slot, got, 0.0)
    flows_full = jnp.concatenate(flow_slots, axis=2) / n_chan

    base_terms = flows_full + q_full.astype(jnp.float32) * 0.125
    split = n_chan == 2
    if split:
        base_terms = lax.dynamic_slice_in_dim(base_terms, own_index, 1, 1)
    comps = base_terms.shape[1]

    def chain_local(incoming):
        src = incoming
        outs = []
        for local_sec in range(sec_local):
            src = base_terms[local_sec] + sample(
                jnp.pad(src, ((0, 0), (4, 4), (4, 4))), q_full[local_sec], 4
            )
            outs.append(src)
        return outs

    outs = chain_local(jnp.zeros((comps, total_rows, columns), jnp.float32))
    pending = list(range(1, len(pieces)))
    for turn in range(1, n_sec):
        carry = outs[-1]
        if pending:
            slot = pending.pop(0)
            carry, warp_inputs[slot] = lax.optimization_barrier((carry, warp_inputs[slot]))
        incoming = shifted_from(carry, ("sec",), (n_sec,), (1,))
        outs = chain_local(incoming)
    warped_pieces = [
        sample(jnp.pad(src, ((0, 0), (0, 0), (4, 4))), offsets[l], 4).astype(jnp.bfloat16)
        for src, (l, _, _) in zip(warp_inputs, pieces)
    ]
    warped = jnp.stack(
        [
            jnp.concatenate([w for w, p in zip(warped_pieces, pieces) if p[0] == l], axis=0)
            for l in range(sec_local)
        ]
    )
    composed = jnp.stack(
        [lax.dynamic_slice_in_dim(o, strip_first, strip_rows, 1) for o in outs]
    )
    if split:
        other = shifted_from(composed, ("chan",), (n_chan,), (1,), cyclic=True)
        composed = jnp.where(
            own_index == 0,
            jnp.concatenate([composed, other], axis=1),
            jnp.concatenate([other, composed], axis=1),
        )
    return (warped, composed)


def solution(mesh):
    in_specs = (
        P(("groups", "sec"), "strip", None),
        P(),
        P(),
        P(("groups", "sec"), None, "strip", None),
    )
    out_specs = (
        P(("groups", "sec"), "chan", "strip", None),
        P(("groups", "sec"), None, "strip", None),
    )
    return jax.shard_map(local, mesh=mesh, in_specs=in_specs, out_specs=out_specs, check_vma=False)
```

```python
import jax
import jax.numpy as jnp
from jax import lax
from jax.sharding import PartitionSpec as P

score_scale = 4.0


def shifted_from(value, axes, sizes, deltas, cyclic=False):
    pairs = []
    counts = [int(s) for s in sizes]
    total = 1
    for c in counts:
        total *= c
    for dst in range(total):
        coords = []
        rem = dst
        for c in reversed(counts):
            coords.append(rem % c)
            rem //= c
        coords = coords[::-1]
        src_coords = []
        ok = True
        for coord, c, d in zip(coords, counts, deltas):
            s = coord - d
            if cyclic:
                s %= c
            elif s < 0 or s >= c:
                ok = False
            src_coords.append(s)
        if not ok:
            continue
        src = 0
        for s, c in zip(src_coords, counts):
            src = src * c + s
        if src != dst:
            pairs.append((src, dst))
    if not pairs:
        return jnp.zeros_like(value)
    return lax.ppermute(value, axes if len(axes) > 1 else axes[0], pairs)


def first_taps(extended, rows_out, row_start):
    columns = extended.shape[-1]
    padded = jnp.pad(extended, ((0, 0), (0, 0), (2, 2)))
    tap_list = []
    for shift_y in (-2, 0, 2):
        for shift_x in (-2, 0, 2):
            tap_list.append(
                padded[
                    :,
                    row_start + shift_y : row_start + shift_y + rows_out,
                    2 + shift_x : 2 + shift_x + columns,
                ]
            )
    return jnp.stack(tap_list)


def second_terms(weights, inputs):
    rows_out = inputs.shape[2] - 2
    columns = inputs.shape[3]
    padded = jnp.pad(inputs, ((0, 0), (0, 0), (0, 0), (1, 1)))
    summed = None
    tap_index = 0
    for shift_y in (-1, 0, 1):
        for shift_x in (-1, 0, 1):
            window = padded[
                :, :, 1 + shift_y : 1 + shift_y + rows_out, 1 + shift_x : 1 + shift_x + columns
            ]
            tap_term = jnp.einsum(
                "oi,ispw->ospw", weights[tap_index], window, preferred_element_type=jnp.float32
            )
            summed = tap_term if summed is None else summed + tap_term
            tap_index += 1
    return summed


def hat_weights(quant_row):
    base = jnp.floor_divide(quant_row, 8)
    frac = (quant_row - 8 * base).astype(jnp.float32) * 0.125
    return [
        jnp.where(base == shift, 1.0 - frac, 0.0) + jnp.where(base + 1 == shift, frac, 0.0)
        for shift in range(-4, 5)
    ]


def sample(source, quant, row_start):
    rows_out, columns = (quant.shape[1], quant.shape[2])
    hats_y = hat_weights(quant[0])
    hats_x = hat_weights(quant[1])
    summed = jnp.zeros((source.shape[0], rows_out, columns), jnp.float32)
    for index_x in range(9):
        inner = jnp.zeros((source.shape[0], rows_out, columns), jnp.float32)
        for index_y in range(9):
            lower = row_start + index_y - 4
            window = source[:, lower : lower + rows_out, index_x : index_x + columns].astype(
                jnp.float32
            )
            inner = inner + hats_y[index_y] * window
        summed = summed + hats_x[index_x] * inner
    return summed


def local(sections, w_first, w_second, offsets):
    sec_local, strip_rows, columns = sections.shape
    n_sec = lax.axis_size("sec")
    n_strip = lax.axis_size("strip")
    n_chan = lax.axis_size("chan")
    strip_index = lax.axis_index("strip")
    own_index = lax.axis_index("chan")
    head_width = w_second.shape[1] // n_chan
    strip_first = strip_index * strip_rows
    total_rows = strip_rows * n_strip
    halo = 7
    ss = ("sec", "strip")
    ss_sizes = (n_sec, n_strip)

    if n_strip == 2:
        packed = jnp.concatenate(
            [sections[:, None].astype(jnp.float32), offsets.astype(jnp.float32)], axis=1
        ).astype(jnp.bfloat16)
        partner = shifted_from(packed, ("strip",), (n_strip,), (1,), cyclic=True)
        other_sec = partner[:, 0]
        from_left = jnp.where(strip_index == 1, other_sec[:, strip_rows - halo :], 0.0)
        from_right = jnp.where(strip_index == 0, other_sec[:, :halo], 0.0)
        other_q = partner[:, 1:].astype(jnp.int32)
        q_full = jnp.where(
            strip_index == 0,
            jnp.concatenate([offsets, other_q], axis=2),
            jnp.concatenate([other_q, offsets], axis=2),
        )
    else:
        from_left = shifted_from(sections[:, strip_rows - halo :], ("strip",), (n_strip,), (1,))
        from_right = shifted_from(sections[:, :halo], ("strip",), (n_strip,), (-1,))
        offset_parts = [offsets]
        for k in range(1, n_strip):
            offset_parts.append(shifted_from(offsets, ("strip",), (n_strip,), (k,), cyclic=True))
        offset_rows = []
        for slot in range(n_strip):
            piece = offset_parts[0]
            for k in range(1, n_strip):
                piece = jnp.where((strip_index - k) % n_strip == slot, offset_parts[k], piece)
            offset_rows.append(piece)
        q_full = jnp.concatenate(offset_rows, axis=2)
    own_ext = jnp.concatenate([from_left, sections, from_right], axis=1)
    prev_ext = shifted_from(own_ext[sec_local - 1 :], ("sec",), (n_sec,), (1,))

    first_rows = strip_rows + 10
    global_rows = strip_first - 5 + lax.broadcasted_iota(jnp.int32, (first_rows, 1), 0)
    inside = (global_rows >= 0) & (global_rows < total_rows)
    feat_rows = global_rows[1:-1]
    feat_inside = (feat_rows >= 0) & (feat_rows < total_rows)
    w_outputs = lax.dynamic_slice_in_dim(w_second, own_index * head_width, head_width, 1)
    w_taps = w_first.astype(jnp.float32)

    def features_of(ext):
        padded = jnp.pad(ext, ((0, 0), (0, 0), (2, 2))).astype(jnp.float32)
        windows = [
            padded[:, 2 + shift_y : 2 + shift_y + first_rows, 2 + shift_x : 2 + shift_x + columns]
            for shift_y in (-2, 0, 2)
            for shift_x in (-2, 0, 2)
        ]
        windows = lax.optimization_barrier(windows)
        maps = None
        for tap_index, window in enumerate(windows):
            term = w_taps[:, tap_index, None, None, None] * window[None]
            maps = term if maps is None else maps + term
        maps = jnp.where(inside, jnp.maximum(maps, 0.0), 0.0).astype(jnp.bfloat16)
        mixed = second_terms(w_outputs, maps)
        return jnp.where(feat_inside, jnp.maximum(mixed, 0.0), 0.0).astype(jnp.bfloat16)

    framed = features_of(jnp.concatenate([prev_ext, own_ext], axis=0))

    current = framed[:, 1:, 4 : 4 + strip_rows, :]
    earlier = jnp.pad(framed[:, :sec_local], ((0, 0), (0, 0), (0, 0), (4, 4)))
    factor = score_scale / head_width
    field_shape = (sec_local, strip_rows, columns)
    running_max = jnp.full(field_shape, -1e30, jnp.float32)
    weight_sum = jnp.zeros(field_shape, jnp.float32)
    along_y = jnp.zeros(field_shape, jnp.float32)
    along_x = jnp.zeros(field_shape, jnp.float32)
    step_cols = lax.broadcasted_iota(jnp.float32, (9, 1, 1, 1), 0) - 4.0
    for shift_y in range(9):
        scores = (
            jnp.stack(
                [
                    jnp.einsum(
                        "cspw,cspw->spw",
                        current,
                        earlier[:, :, shift_y : shift_y + strip_rows, shift_x : shift_x + columns],
                        preferred_element_type=jnp.float32,
                    )
                    for shift_x in range(9)
                ]
            )
            * factor
        )
        highest = jnp.maximum(running_max, jnp.max(scores, axis=0))
        rescale = jnp.exp(running_max - highest)
        weights = jnp.exp(scores - highest)
        block_sum = jnp.sum(weights, axis=0)
        weight_sum = weight_sum * rescale + block_sum
        along_y = along_y * rescale + (shift_y - 4.0) * block_sum
        along_x = along_x * rescale + jnp.sum(weights * step_cols, axis=0)
        running_max = highest
    head_flow = jnp.stack([along_y / weight_sum, along_x / weight_sum], axis=1)

    pieces = [(0, 0, head_width)]
    chain_slots = max(n_sec - 1, 1)
    rest = sec_local - 1
    per_sec = max(1, -(-chain_slots // max(rest, 1))) if rest else 0
    for local_sec in range(1, sec_local):
        bounds = [round(head_width * k / per_sec) for k in range(per_sec + 1)]
        for lo_c, hi_c in zip(bounds[:-1], bounds[1:]):
            pieces.append((local_sec, lo_c, hi_c))
    warp_inputs = [framed[lo_c:hi_c, l + 1] for l, lo_c, hi_c in pieces]
    head_flow, warp_inputs[0] = lax.optimization_barrier((head_flow, warp_inputs[0]))

    sc = ("strip", "chan")
    sc_sizes = (n_strip, n_chan)
    flow_slots = [jnp.zeros_like(head_flow) for _ in range(n_strip)]
    for k in range(n_strip * n_chan):
        if k == 0:
            got = head_flow
        else:
            got = shifted_from(head_flow, sc, sc_sizes, (k // n_chan, k % n_chan), cyclic=True)
        src_strip = (strip_index - k // n_chan) % n_strip
        for slot in range(n_strip):
            flow_slots[slot] = flow_slots[slot] + jnp.where(src_strip == slot, got, 0.0)
    flows_full = jnp.concatenate(flow_slots, axis=2) / n_chan

    base_terms = flows_full + q_full.astype(jnp.float32) * 0.125
    split = n_chan == 2
    if split:
        base_terms = lax.dynamic_slice_in_dim(base_terms, own_index, 1, 1)
    comps = base_terms.shape[1]

    def chain_local(incoming):
        src = incoming
        outs = []
        for local_sec in range(sec_local):
            src = base_terms[local_sec] + sample(
                jnp.pad(src, ((0, 0), (4, 4), (4, 4))), q_full[local_sec], 4
            )
            outs.append(src)
        return outs

    outs = chain_local(jnp.zeros((comps, total_rows, columns), jnp.float32))
    pending = list(range(1, len(pieces)))
    for turn in range(1, n_sec):
        carry = outs[-1]
        if pending:
            slot = pending.pop(0)
            carry, warp_inputs[slot] = lax.optimization_barrier((carry, warp_inputs[slot]))
        incoming = shifted_from(carry, ("sec",), (n_sec,), (1,))
        outs = chain_local(incoming)
    warped_pieces = [
        sample(jnp.pad(src, ((0, 0), (0, 0), (4, 4))), offsets[l], 4).astype(jnp.bfloat16)
        for src, (l, _, _) in zip(warp_inputs, pieces)
    ]
    warped = jnp.stack(
        [
            jnp.concatenate([w for w, p in zip(warped_pieces, pieces) if p[0] == l], axis=0)
            for l in range(sec_local)
        ]
    )
    composed = jnp.stack(
        [lax.dynamic_slice_in_dim(o, strip_first, strip_rows, 1) for o in outs]
    )
    if split:
        other = shifted_from(composed, ("chan",), (n_chan,), (1,), cyclic=True)
        composed = jnp.where(
            own_index == 0,
            jnp.concatenate([composed, other], axis=1),
            jnp.concatenate([other, composed], axis=1),
        )
    return (warped, composed)


def solution(mesh):
    in_specs = (
        P(("groups", "sec"), "strip", None),
        P(),
        P(),
        P(("groups", "sec"), None, "strip", None),
    )
    out_specs = (
        P(("groups", "sec"), "chan", "strip", None),
        P(("groups", "sec"), None, "strip", None),
    )
    return jax.shard_map(local, mesh=mesh, in_specs=in_specs, out_specs=out_specs, check_vma=False)
```

```python
import jax
import jax.numpy as jnp
from jax import lax
from jax.sharding import PartitionSpec as P

score_scale = 4.0


def shifted_from(value, axes, sizes, deltas, cyclic=False):
    pairs = []
    counts = [int(s) for s in sizes]
    total = 1
    for c in counts:
        total *= c
    for dst in range(total):
        coords = []
        rem = dst
        for c in reversed(counts):
            coords.append(rem % c)
            rem //= c
        coords = coords[::-1]
        src_coords = []
        ok = True
        for coord, c, d in zip(coords, counts, deltas):
            s = coord - d
            if cyclic:
                s %= c
            elif s < 0 or s >= c:
                ok = False
            src_coords.append(s)
        if not ok:
            continue
        src = 0
        for s, c in zip(src_coords, counts):
            src = src * c + s
        if src != dst:
            pairs.append((src, dst))
    if not pairs:
        return jnp.zeros_like(value)
    return lax.ppermute(value, axes if len(axes) > 1 else axes[0], pairs)


def first_taps(extended, rows_out, row_start):
    columns = extended.shape[-1]
    padded = jnp.pad(extended, ((0, 0), (0, 0), (2, 2)))
    tap_list = []
    for shift_y in (-2, 0, 2):
        for shift_x in (-2, 0, 2):
            tap_list.append(
                padded[
                    :,
                    row_start + shift_y : row_start + shift_y + rows_out,
                    2 + shift_x : 2 + shift_x + columns,
                ]
            )
    return jnp.stack(tap_list)


def second_terms(weights, inputs):
    rows_out = inputs.shape[2] - 2
    columns = inputs.shape[3]
    padded = jnp.pad(inputs, ((0, 0), (0, 0), (0, 0), (1, 1)))
    summed = None
    tap_index = 0
    for shift_y in (-1, 0, 1):
        for shift_x in (-1, 0, 1):
            window = padded[
                :, :, 1 + shift_y : 1 + shift_y + rows_out, 1 + shift_x : 1 + shift_x + columns
            ]
            tap_term = jnp.einsum(
                "oi,ispw->ospw", weights[tap_index], window, preferred_element_type=jnp.float32
            )
            summed = tap_term if summed is None else summed + tap_term
            tap_index += 1
    return summed


def hat_weights(quant_row):
    base = jnp.floor_divide(quant_row, 8)
    frac = (quant_row - 8 * base).astype(jnp.float32) * 0.125
    return [
        jnp.where(base == shift, 1.0 - frac, 0.0) + jnp.where(base + 1 == shift, frac, 0.0)
        for shift in range(-4, 5)
    ]


def sample(source, quant, row_start):
    rows_out, columns = (quant.shape[1], quant.shape[2])
    hats_y = hat_weights(quant[0])
    hats_x = hat_weights(quant[1])
    summed = jnp.zeros((source.shape[0], rows_out, columns), jnp.float32)
    for index_x in range(9):
        inner = jnp.zeros((source.shape[0], rows_out, columns), jnp.float32)
        for index_y in range(9):
            lower = row_start + index_y - 4
            window = source[:, lower : lower + rows_out, index_x : index_x + columns].astype(
                jnp.float32
            )
            inner = inner + hats_y[index_y] * window
        summed = summed + hats_x[index_x] * inner
    return summed


def local(sections, w_first, w_second, offsets):
    sec_local, strip_rows, columns = sections.shape
    n_sec = lax.axis_size("sec")
    n_strip = lax.axis_size("strip")
    n_chan = lax.axis_size("chan")
    strip_index = lax.axis_index("strip")
    own_index = lax.axis_index("chan")
    head_width = w_second.shape[1] // n_chan
    strip_first = strip_index * strip_rows
    total_rows = strip_rows * n_strip
    halo = 7
    ss = ("sec", "strip")
    ss_sizes = (n_sec, n_strip)

    if n_strip == 2:
        packed = jnp.concatenate(
            [sections[:, None].astype(jnp.float32), offsets.astype(jnp.float32)], axis=1
        ).astype(jnp.bfloat16)
        partner = shifted_from(packed, ("strip",), (n_strip,), (1,), cyclic=True)
        other_sec = partner[:, 0]
        from_left = jnp.where(strip_index == 1, other_sec[:, strip_rows - halo :], 0.0)
        from_right = jnp.where(strip_index == 0, other_sec[:, :halo], 0.0)
        other_q = partner[:, 1:].astype(jnp.int32)
        q_full = jnp.where(
            strip_index == 0,
            jnp.concatenate([offsets, other_q], axis=2),
            jnp.concatenate([other_q, offsets], axis=2),
        )
    else:
        from_left = shifted_from(sections[:, strip_rows - halo :], ("strip",), (n_strip,), (1,))
        from_right = shifted_from(sections[:, :halo], ("strip",), (n_strip,), (-1,))
        offset_parts = [offsets]
        for k in range(1, n_strip):
            offset_parts.append(shifted_from(offsets, ("strip",), (n_strip,), (k,), cyclic=True))
        offset_rows = []
        for slot in range(n_strip):
            piece = offset_parts[0]
            for k in range(1, n_strip):
                piece = jnp.where((strip_index - k) % n_strip == slot, offset_parts[k], piece)
            offset_rows.append(piece)
        q_full = jnp.concatenate(offset_rows, axis=2)
    own_ext = jnp.concatenate([from_left, sections, from_right], axis=1)
    prev_ext = shifted_from(own_ext[sec_local - 1 :], ("sec",), (n_sec,), (1,))

    first_rows = strip_rows + 10
    global_rows = strip_first - 5 + lax.broadcasted_iota(jnp.int32, (first_rows, 1), 0)
    inside = (global_rows >= 0) & (global_rows < total_rows)
    feat_rows = global_rows[1:-1]
    feat_inside = (feat_rows >= 0) & (feat_rows < total_rows)
    w_outputs = lax.dynamic_slice_in_dim(w_second, own_index * head_width, head_width, 1)
    w_taps = w_first.astype(jnp.float32)

    def features_of(ext):
        padded = jnp.pad(ext, ((0, 0), (0, 0), (2, 2))).astype(jnp.float32)
        maps = None
        tap_index = 0
        for shift_y in (-2, 0, 2):
            for shift_x in (-2, 0, 2):
                window = padded[:, 2 + shift_y : 2 + shift_y + first_rows, 2 + shift_x : 2 + shift_x + columns]
                term = w_taps[:, tap_index, None, None, None] * window[None]
                maps = term if maps is None else maps + term
                tap_index += 1
        maps = jnp.where(inside, jnp.maximum(maps, 0.0), 0.0).astype(jnp.bfloat16)
        mixed = second_terms(w_outputs, maps)
        return jnp.where(feat_inside, jnp.maximum(mixed, 0.0), 0.0).astype(jnp.bfloat16)

    framed = features_of(jnp.concatenate([prev_ext, own_ext], axis=0))

    current = framed[:, 1:, 4 : 4 + strip_rows, :]
    earlier = jnp.pad(framed[:, :sec_local], ((0, 0), (0, 0), (0, 0), (4, 4)))
    factor = score_scale / head_width
    field_shape = (sec_local, strip_rows, columns)
    running_max = jnp.full(field_shape, -1e30, jnp.float32)
    weight_sum = jnp.zeros(field_shape, jnp.float32)
    along_y = jnp.zeros(field_shape, jnp.float32)
    along_x = jnp.zeros(field_shape, jnp.float32)
    step_cols = lax.broadcasted_iota(jnp.float32, (9, 1, 1, 1), 0) - 4.0
    for shift_y in range(9):
        scores = (
            jnp.stack(
                [
                    jnp.einsum(
                        "cspw,cspw->spw",
                        current,
                        earlier[:, :, shift_y : shift_y + strip_rows, shift_x : shift_x + columns],
                        preferred_element_type=jnp.float32,
                    )
                    for shift_x in range(9)
                ]
            )
            * factor
        )
        highest = jnp.maximum(running_max, jnp.max(scores, axis=0))
        rescale = jnp.exp(running_max - highest)
        weights = jnp.exp(scores - highest)
        block_sum = jnp.sum(weights, axis=0)
        weight_sum = weight_sum * rescale + block_sum
        along_y = along_y * rescale + (shift_y - 4.0) * block_sum
        along_x = along_x * rescale + jnp.sum(weights * step_cols, axis=0)
        running_max = highest
    head_flow = jnp.stack([along_y / weight_sum, along_x / weight_sum], axis=1)

    pieces = [(0, 0, head_width)]
    chain_slots = max(n_sec - 1, 1)
    rest = sec_local - 1
    per_sec = max(1, -(-chain_slots // max(rest, 1))) if rest else 0
    for local_sec in range(1, sec_local):
        bounds = [round(head_width * k / per_sec) for k in range(per_sec + 1)]
        for lo_c, hi_c in zip(bounds[:-1], bounds[1:]):
            pieces.append((local_sec, lo_c, hi_c))
    warp_inputs = [framed[lo_c:hi_c, l + 1] for l, lo_c, hi_c in pieces]
    head_flow, warp_inputs[0] = lax.optimization_barrier((head_flow, warp_inputs[0]))

    sc = ("strip", "chan")
    sc_sizes = (n_strip, n_chan)
    flow_slots = [jnp.zeros_like(head_flow) for _ in range(n_strip)]
    for k in range(n_strip * n_chan):
        if k == 0:
            got = head_flow
        else:
            got = shifted_from(head_flow, sc, sc_sizes, (k // n_chan, k % n_chan), cyclic=True)
        src_strip = (strip_index - k // n_chan) % n_strip
        for slot in range(n_strip):
            flow_slots[slot] = flow_slots[slot] + jnp.where(src_strip == slot, got, 0.0)
    flows_full = jnp.concatenate(flow_slots, axis=2) / n_chan

    base_terms = flows_full + q_full.astype(jnp.float32) * 0.125
    split = n_chan == 2
    if split:
        base_terms = lax.dynamic_slice_in_dim(base_terms, own_index, 1, 1)
    comps = base_terms.shape[1]

    packet = jnp.concatenate([base_terms, q_full.astype(jnp.float32)], axis=1)
    tied = lax.optimization_barrier((packet, warp_inputs[1:]))
    packet, warp_inputs[1:] = tied[0], list(tied[1])
    gathered = [shifted_from(packet, ("sec",), (n_sec,), (k,)) for k in range(n_sec - 1, 0, -1)]
    slots = jnp.concatenate(gathered + [packet], axis=0)
    src = jnp.zeros((comps, total_rows, columns), jnp.float32)
    outs = []
    for slot in range(slots.shape[0]):
        quant = slots[slot, comps:].astype(jnp.int32)
        src = slots[slot, :comps] + sample(jnp.pad(src, ((0, 0), (4, 4), (4, 4))), quant, 4)
        outs.append(src)
    outs = outs[len(outs) - sec_local :]
    warped_pieces = [
        sample(jnp.pad(src, ((0, 0), (0, 0), (4, 4))), offsets[l], 4).astype(jnp.bfloat16)
        for src, (l, _, _) in zip(warp_inputs, pieces)
    ]
    warped = jnp.stack(
        [
            jnp.concatenate([w for w, p in zip(warped_pieces, pieces) if p[0] == l], axis=0)
            for l in range(sec_local)
        ]
    )
    composed = jnp.stack(
        [lax.dynamic_slice_in_dim(o, strip_first, strip_rows, 1) for o in outs]
    )
    if split:
        other = shifted_from(composed, ("chan",), (n_chan,), (1,), cyclic=True)
        composed = jnp.where(
            own_index == 0,
            jnp.concatenate([composed, other], axis=1),
            jnp.concatenate([other, composed], axis=1),
        )
    return (warped, composed)


def solution(mesh):
    in_specs = (
        P(("groups", "sec"), "strip", None),
        P(),
        P(),
        P(("groups", "sec"), None, "strip", None),
    )
    out_specs = (
        P(("groups", "sec"), "chan", "strip", None),
        P(("groups", "sec"), None, "strip", None),
    )
    return jax.shard_map(local, mesh=mesh, in_specs=in_specs, out_specs=out_specs, check_vma=False)
```

```python
import jax
import jax.numpy as jnp
from jax import lax
from jax.sharding import PartitionSpec as P

score_scale = 4.0


def shifted_from(value, axes, sizes, deltas, cyclic=False):
    pairs = []
    counts = [int(s) for s in sizes]
    total = 1
    for c in counts:
        total *= c
    for dst in range(total):
        coords = []
        rem = dst
        for c in reversed(counts):
            coords.append(rem % c)
            rem //= c
        coords = coords[::-1]
        src_coords = []
        ok = True
        for coord, c, d in zip(coords, counts, deltas):
            s = coord - d
            if cyclic:
                s %= c
            elif s < 0 or s >= c:
                ok = False
            src_coords.append(s)
        if not ok:
            continue
        src = 0
        for s, c in zip(src_coords, counts):
            src = src * c + s
        if src != dst:
            pairs.append((src, dst))
    if not pairs:
        return jnp.zeros_like(value)
    return lax.ppermute(value, axes if len(axes) > 1 else axes[0], pairs)


def first_taps(extended, rows_out, row_start):
    columns = extended.shape[-1]
    padded = jnp.pad(extended, ((0, 0), (0, 0), (2, 2)))
    tap_list = []
    for shift_y in (-2, 0, 2):
        for shift_x in (-2, 0, 2):
            tap_list.append(
                padded[
                    :,
                    row_start + shift_y : row_start + shift_y + rows_out,
                    2 + shift_x : 2 + shift_x + columns,
                ]
            )
    return jnp.stack(tap_list)


def second_terms(weights, inputs):
    rows_out = inputs.shape[2] - 2
    columns = inputs.shape[3]
    padded = jnp.pad(inputs, ((0, 0), (0, 0), (0, 0), (1, 1)))
    summed = None
    tap_index = 0
    for shift_y in (-1, 0, 1):
        for shift_x in (-1, 0, 1):
            window = padded[
                :, :, 1 + shift_y : 1 + shift_y + rows_out, 1 + shift_x : 1 + shift_x + columns
            ]
            tap_term = jnp.einsum(
                "oi,ispw->ospw", weights[tap_index], window, preferred_element_type=jnp.float32
            )
            summed = tap_term if summed is None else summed + tap_term
            tap_index += 1
    return summed


def hat_weights(quant_row):
    base = jnp.floor_divide(quant_row, 8)
    frac = (quant_row - 8 * base).astype(jnp.float32) * 0.125
    return [
        jnp.where(base == shift, 1.0 - frac, 0.0) + jnp.where(base + 1 == shift, frac, 0.0)
        for shift in range(-4, 5)
    ]


def sample(source, quant, row_start):
    return sample_hats(source, hat_weights(quant[0]), hat_weights(quant[1]), row_start)


def sample_hats(source, hats_y, hats_x, row_start):
    rows_out, columns = hats_y[0].shape
    summed = jnp.zeros((source.shape[0], rows_out, columns), jnp.float32)
    for index_x in range(9):
        inner = jnp.zeros((source.shape[0], rows_out, columns), jnp.float32)
        for index_y in range(9):
            lower = row_start + index_y - 4
            window = source[:, lower : lower + rows_out, index_x : index_x + columns].astype(
                jnp.float32
            )
            inner = inner + hats_y[index_y] * window
        summed = summed + hats_x[index_x] * inner
    return summed


def local(sections, w_first, w_second, offsets):
    sec_local, strip_rows, columns = sections.shape
    n_sec = lax.axis_size("sec")
    n_strip = lax.axis_size("strip")
    n_chan = lax.axis_size("chan")
    strip_index = lax.axis_index("strip")
    own_index = lax.axis_index("chan")
    head_width = w_second.shape[1] // n_chan
    strip_first = strip_index * strip_rows
    total_rows = strip_rows * n_strip
    halo = 7
    ss = ("sec", "strip")
    ss_sizes = (n_sec, n_strip)

    if n_strip == 2:
        packed = jnp.concatenate(
            [sections[:, None].astype(jnp.float32), offsets.astype(jnp.float32)], axis=1
        ).astype(jnp.bfloat16)
        partner = shifted_from(packed, ("strip",), (n_strip,), (1,), cyclic=True)
        other_sec = partner[:, 0]
        from_left = jnp.where(strip_index == 1, other_sec[:, strip_rows - halo :], 0.0)
        from_right = jnp.where(strip_index == 0, other_sec[:, :halo], 0.0)
        other_q = partner[:, 1:].astype(jnp.int32)
        q_full = jnp.where(
            strip_index == 0,
            jnp.concatenate([offsets, other_q], axis=2),
            jnp.concatenate([other_q, offsets], axis=2),
        )
    else:
        from_left = shifted_from(sections[:, strip_rows - halo :], ("strip",), (n_strip,), (1,))
        from_right = shifted_from(sections[:, :halo], ("strip",), (n_strip,), (-1,))
        offset_parts = [offsets]
        for k in range(1, n_strip):
            offset_parts.append(shifted_from(offsets, ("strip",), (n_strip,), (k,), cyclic=True))
        offset_rows = []
        for slot in range(n_strip):
            piece = offset_parts[0]
            for k in range(1, n_strip):
                piece = jnp.where((strip_index - k) % n_strip == slot, offset_parts[k], piece)
            offset_rows.append(piece)
        q_full = jnp.concatenate(offset_rows, axis=2)
    own_ext = jnp.concatenate([from_left, sections, from_right], axis=1)
    prev_ext = shifted_from(own_ext[sec_local - 1 :], ("sec",), (n_sec,), (1,))

    first_rows = strip_rows + 10
    global_rows = strip_first - 5 + lax.broadcasted_iota(jnp.int32, (first_rows, 1), 0)
    inside = (global_rows >= 0) & (global_rows < total_rows)
    feat_rows = global_rows[1:-1]
    feat_inside = (feat_rows >= 0) & (feat_rows < total_rows)
    w_outputs = lax.dynamic_slice_in_dim(w_second, own_index * head_width, head_width, 1)
    w_taps = w_first.astype(jnp.float32)

    def features_of(ext):
        padded = jnp.pad(ext, ((0, 0), (0, 0), (2, 2))).astype(jnp.float32)
        windows = [
            padded[:, 2 + shift_y : 2 + shift_y + first_rows, 2 + shift_x : 2 + shift_x + columns]
            for shift_y in (-2, 0, 2)
            for shift_x in (-2, 0, 2)
        ]
        windows = lax.optimization_barrier(windows)
        maps = None
        for tap_index, window in enumerate(windows):
            term = w_taps[:, tap_index, None, None, None] * window[None]
            maps = term if maps is None else maps + term
        maps = jnp.where(inside, jnp.maximum(maps, 0.0), 0.0).astype(jnp.bfloat16)
        mixed = second_terms(w_outputs, maps)
        return jnp.where(feat_inside, jnp.maximum(mixed, 0.0), 0.0).astype(jnp.bfloat16)

    framed = features_of(jnp.concatenate([prev_ext, own_ext], axis=0))

    current = framed[:, 1:, 4 : 4 + strip_rows, :]
    earlier = jnp.pad(framed[:, :sec_local], ((0, 0), (0, 0), (0, 0), (4, 4)))
    factor = score_scale / head_width
    field_shape = (sec_local, strip_rows, columns)
    running_max = jnp.full(field_shape, -1e30, jnp.float32)
    weight_sum = jnp.zeros(field_shape, jnp.float32)
    along_y = jnp.zeros(field_shape, jnp.float32)
    along_x = jnp.zeros(field_shape, jnp.float32)
    step_cols = lax.broadcasted_iota(jnp.float32, (9, 1, 1, 1), 0) - 4.0
    for shift_y in range(9):
        scores = (
            jnp.stack(
                [
                    jnp.einsum(
                        "cspw,cspw->spw",
                        current,
                        earlier[:, :, shift_y : shift_y + strip_rows, shift_x : shift_x + columns],
                        preferred_element_type=jnp.float32,
                    )
                    for shift_x in range(9)
                ]
            )
            * factor
        )
        highest = jnp.maximum(running_max, jnp.max(scores, axis=0))
        rescale = jnp.exp(running_max - highest)
        weights = jnp.exp(scores - highest)
        block_sum = jnp.sum(weights, axis=0)
        weight_sum = weight_sum * rescale + block_sum
        along_y = along_y * rescale + (shift_y - 4.0) * block_sum
        along_x = along_x * rescale + jnp.sum(weights * step_cols, axis=0)
        running_max = highest
    head_flow = jnp.stack([along_y / weight_sum, along_x / weight_sum], axis=1)

    pieces = [(0, 0, head_width)]
    chain_slots = max(n_sec - 1, 1)
    rest = sec_local - 1
    per_sec = max(1, -(-chain_slots // max(rest, 1))) if rest else 0
    for local_sec in range(1, sec_local):
        bounds = [round(head_width * k / per_sec) for k in range(per_sec + 1)]
        for lo_c, hi_c in zip(bounds[:-1], bounds[1:]):
            pieces.append((local_sec, lo_c, hi_c))
    warp_inputs = [framed[lo_c:hi_c, l + 1] for l, lo_c, hi_c in pieces]
    head_flow, warp_inputs[0] = lax.optimization_barrier((head_flow, warp_inputs[0]))

    sc = ("strip", "chan")
    sc_sizes = (n_strip, n_chan)
    flow_slots = [jnp.zeros_like(head_flow) for _ in range(n_strip)]
    for k in range(n_strip * n_chan):
        if k == 0:
            got = head_flow
        else:
            got = shifted_from(head_flow, sc, sc_sizes, (k // n_chan, k % n_chan), cyclic=True)
        src_strip = (strip_index - k // n_chan) % n_strip
        for slot in range(n_strip):
            flow_slots[slot] = flow_slots[slot] + jnp.where(src_strip == slot, got, 0.0)
    flows_full = jnp.concatenate(flow_slots, axis=2) / n_chan

    base_terms = flows_full + q_full.astype(jnp.float32) * 0.125
    split = n_chan == 2
    if split:
        base_terms = lax.dynamic_slice_in_dim(base_terms, own_index, 1, 1)
    comps = base_terms.shape[1]

    chain_hats = lax.optimization_barrier(
        [(hat_weights(q_full[l, 0]), hat_weights(q_full[l, 1])) for l in range(sec_local)]
    )

    def chain_local(incoming):
        src = incoming
        outs = []
        for local_sec in range(sec_local):
            hats_y, hats_x = chain_hats[local_sec]
            src = base_terms[local_sec] + sample_hats(
                jnp.pad(src, ((0, 0), (4, 4), (4, 4))), hats_y, hats_x, 4
            )
            outs.append(src)
        return outs

    outs = chain_local(jnp.zeros((comps, total_rows, columns), jnp.float32))
    pending = list(range(1, len(pieces)))
    for turn in range(1, n_sec):
        carry = outs[-1]
        if pending:
            slot = pending.pop(0)
            carry, warp_inputs[slot] = lax.optimization_barrier((carry, warp_inputs[slot]))
        incoming = shifted_from(carry, ("sec",), (n_sec,), (1,))
        outs = chain_local(incoming)
    warped_pieces = [
        sample(jnp.pad(src, ((0, 0), (0, 0), (4, 4))), offsets[l], 4).astype(jnp.bfloat16)
        for src, (l, _, _) in zip(warp_inputs, pieces)
    ]
    warped = jnp.stack(
        [
            jnp.concatenate([w for w, p in zip(warped_pieces, pieces) if p[0] == l], axis=0)
            for l in range(sec_local)
        ]
    )
    composed = jnp.stack(
        [lax.dynamic_slice_in_dim(o, strip_first, strip_rows, 1) for o in outs]
    )
    if split:
        other = shifted_from(composed, ("chan",), (n_chan,), (1,), cyclic=True)
        composed = jnp.where(
            own_index == 0,
            jnp.concatenate([composed, other], axis=1),
            jnp.concatenate([other, composed], axis=1),
        )
    return (warped, composed)


def solution(mesh):
    in_specs = (
        P(("groups", "sec"), "strip", None),
        P(),
        P(),
        P(("groups", "sec"), None, "strip", None),
    )
    out_specs = (
        P(("groups", "sec"), "chan", "strip", None),
        P(("groups", "sec"), None, "strip", None),
    )
    return jax.shard_map(local, mesh=mesh, in_specs=in_specs, out_specs=out_specs, check_vma=False)
```

```python
import jax
import jax.numpy as jnp
from jax import lax
from jax.sharding import PartitionSpec as P

score_scale = 4.0


def shifted_from(value, axes, sizes, deltas, cyclic=False):
    pairs = []
    counts = [int(s) for s in sizes]
    total = 1
    for c in counts:
        total *= c
    for dst in range(total):
        coords = []
        rem = dst
        for c in reversed(counts):
            coords.append(rem % c)
            rem //= c
        coords = coords[::-1]
        src_coords = []
        ok = True
        for coord, c, d in zip(coords, counts, deltas):
            s = coord - d
            if cyclic:
                s %= c
            elif s < 0 or s >= c:
                ok = False
            src_coords.append(s)
        if not ok:
            continue
        src = 0
        for s, c in zip(src_coords, counts):
            src = src * c + s
        if src != dst:
            pairs.append((src, dst))
    if not pairs:
        return jnp.zeros_like(value)
    return lax.ppermute(value, axes if len(axes) > 1 else axes[0], pairs)


def first_taps(extended, rows_out, row_start):
    columns = extended.shape[-1]
    padded = jnp.pad(extended, ((0, 0), (0, 0), (2, 2)))
    tap_list = []
    for shift_y in (-2, 0, 2):
        for shift_x in (-2, 0, 2):
            tap_list.append(
                padded[
                    :,
                    row_start + shift_y : row_start + shift_y + rows_out,
                    2 + shift_x : 2 + shift_x + columns,
                ]
            )
    return jnp.stack(tap_list)


def second_terms(weights, inputs):
    rows_out = inputs.shape[2] - 2
    columns = inputs.shape[3]
    padded = jnp.pad(inputs, ((0, 0), (0, 0), (0, 0), (1, 1)))
    summed = None
    tap_index = 0
    for shift_y in (-1, 0, 1):
        for shift_x in (-1, 0, 1):
            window = padded[
                :, :, 1 + shift_y : 1 + shift_y + rows_out, 1 + shift_x : 1 + shift_x + columns
            ]
            tap_term = jnp.einsum(
                "oi,ispw->ospw", weights[tap_index], window, preferred_element_type=jnp.float32
            )
            summed = tap_term if summed is None else summed + tap_term
            tap_index += 1
    return summed


def hat_weights(quant_row):
    base = jnp.floor_divide(quant_row, 8)
    frac = (quant_row - 8 * base).astype(jnp.float32) * 0.125
    return [
        jnp.where(base == shift, 1.0 - frac, 0.0) + jnp.where(base + 1 == shift, frac, 0.0)
        for shift in range(-4, 5)
    ]


def sample(source, quant, row_start):
    rows_out, columns = (quant.shape[1], quant.shape[2])
    hats_y = hat_weights(quant[0])
    hats_x = hat_weights(quant[1])
    summed = jnp.zeros((source.shape[0], rows_out, columns), jnp.float32)
    for index_x in range(9):
        inner = jnp.zeros((source.shape[0], rows_out, columns), jnp.float32)
        for index_y in range(9):
            lower = row_start + index_y - 4
            window = source[:, lower : lower + rows_out, index_x : index_x + columns].astype(
                jnp.float32
            )
            inner = inner + hats_y[index_y] * window
        summed = summed + hats_x[index_x] * inner
    return summed


def local(sections, w_first, w_second, offsets):
    sec_local, strip_rows, columns = sections.shape
    n_sec = lax.axis_size("sec")
    n_strip = lax.axis_size("strip")
    n_chan = lax.axis_size("chan")
    strip_index = lax.axis_index("strip")
    own_index = lax.axis_index("chan")
    head_width = w_second.shape[1] // n_chan
    strip_first = strip_index * strip_rows
    total_rows = strip_rows * n_strip
    halo = 7
    ss = ("sec", "strip")
    ss_sizes = (n_sec, n_strip)

    if n_strip == 2:
        behind = shifted_from(sections[sec_local - 1 :], ("sec",), (n_sec,), (1,))
        planes = offsets.shape[1] * sec_local
        packed = jnp.concatenate(
            [
                sections.astype(jnp.float32),
                offsets.reshape(planes, strip_rows, columns).astype(jnp.float32),
                behind.astype(jnp.float32),
            ],
            axis=0,
        ).astype(jnp.bfloat16)
        partner = shifted_from(packed, ("strip",), (n_strip,), (1,), cyclic=True)
        other_sec = partner[:sec_local]
        other_q = partner[sec_local : sec_local + planes].astype(jnp.int32).reshape(offsets.shape)
        other_behind = partner[sec_local + planes :]
        from_left = jnp.where(strip_index == 1, other_sec[:, strip_rows - halo :], 0.0)
        from_right = jnp.where(strip_index == 0, other_sec[:, :halo], 0.0)
        prev_left = jnp.where(strip_index == 1, other_behind[:, strip_rows - halo :], 0.0)
        prev_right = jnp.where(strip_index == 0, other_behind[:, :halo], 0.0)
        prev_ext = jnp.concatenate([prev_left, behind, prev_right], axis=1)
        q_full = jnp.where(
            strip_index == 0,
            jnp.concatenate([offsets, other_q], axis=2),
            jnp.concatenate([other_q, offsets], axis=2),
        )
        own_ext = jnp.concatenate([from_left, sections, from_right], axis=1)
    else:
        from_left = shifted_from(sections[:, strip_rows - halo :], ("strip",), (n_strip,), (1,))
        from_right = shifted_from(sections[:, :halo], ("strip",), (n_strip,), (-1,))
        offset_parts = [offsets]
        for k in range(1, n_strip):
            offset_parts.append(shifted_from(offsets, ("strip",), (n_strip,), (k,), cyclic=True))
        offset_rows = []
        for slot in range(n_strip):
            piece = offset_parts[0]
            for k in range(1, n_strip):
                piece = jnp.where((strip_index - k) % n_strip == slot, offset_parts[k], piece)
            offset_rows.append(piece)
        q_full = jnp.concatenate(offset_rows, axis=2)
        own_ext = jnp.concatenate([from_left, sections, from_right], axis=1)
        prev_ext = shifted_from(own_ext[sec_local - 1 :], ("sec",), (n_sec,), (1,))

    first_rows = strip_rows + 10
    global_rows = strip_first - 5 + lax.broadcasted_iota(jnp.int32, (first_rows, 1), 0)
    inside = (global_rows >= 0) & (global_rows < total_rows)
    feat_rows = global_rows[1:-1]
    feat_inside = (feat_rows >= 0) & (feat_rows < total_rows)
    w_outputs = lax.dynamic_slice_in_dim(w_second, own_index * head_width, head_width, 1)
    w_taps = w_first.astype(jnp.float32)

    def features_of(ext):
        padded = jnp.pad(ext, ((0, 0), (0, 0), (2, 2))).astype(jnp.float32)
        windows = [
            padded[:, 2 + shift_y : 2 + shift_y + first_rows, 2 + shift_x : 2 + shift_x + columns]
            for shift_y in (-2, 0, 2)
            for shift_x in (-2, 0, 2)
        ]
        windows = lax.optimization_barrier(windows)
        maps = None
        for tap_index, window in enumerate(windows):
            term = w_taps[:, tap_index, None, None, None] * window[None]
            maps = term if maps is None else maps + term
        maps = jnp.where(inside, jnp.maximum(maps, 0.0), 0.0).astype(jnp.bfloat16)
        mixed = second_terms(w_outputs, maps)
        return jnp.where(feat_inside, jnp.maximum(mixed, 0.0), 0.0).astype(jnp.bfloat16)

    framed = features_of(jnp.concatenate([prev_ext, own_ext], axis=0))

    current = framed[:, 1:, 4 : 4 + strip_rows, :]
    earlier = jnp.pad(framed[:, :sec_local], ((0, 0), (0, 0), (0, 0), (4, 4)))
    factor = score_scale / head_width
    field_shape = (sec_local, strip_rows, columns)
    running_max = jnp.full(field_shape, -1e30, jnp.float32)
    weight_sum = jnp.zeros(field_shape, jnp.float32)
    along_y = jnp.zeros(field_shape, jnp.float32)
    along_x = jnp.zeros(field_shape, jnp.float32)
    step_cols = lax.broadcasted_iota(jnp.float32, (9, 1, 1, 1), 0) - 4.0
    for shift_y in range(9):
        scores = (
            jnp.stack(
                [
                    jnp.einsum(
                        "cspw,cspw->spw",
                        current,
                        earlier[:, :, shift_y : shift_y + strip_rows, shift_x : shift_x + columns],
                        preferred_element_type=jnp.float32,
                    )
                    for shift_x in range(9)
                ]
            )
            * factor
        )
        highest = jnp.maximum(running_max, jnp.max(scores, axis=0))
        rescale = jnp.exp(running_max - highest)
        weights = jnp.exp(scores - highest)
        block_sum = jnp.sum(weights, axis=0)
        weight_sum = weight_sum * rescale + block_sum
        along_y = along_y * rescale + (shift_y - 4.0) * block_sum
        along_x = along_x * rescale + jnp.sum(weights * step_cols, axis=0)
        running_max = highest
    head_flow = jnp.stack([along_y / weight_sum, along_x / weight_sum], axis=1)

    pieces = [(0, 0, head_width)]
    chain_slots = max(n_sec - 1, 1)
    rest = sec_local - 1
    per_sec = max(1, -(-chain_slots // max(rest, 1))) if rest else 0
    for local_sec in range(1, sec_local):
        bounds = [round(head_width * k / per_sec) for k in range(per_sec + 1)]
        for lo_c, hi_c in zip(bounds[:-1], bounds[1:]):
            pieces.append((local_sec, lo_c, hi_c))
    warp_inputs = [framed[lo_c:hi_c, l + 1] for l, lo_c, hi_c in pieces]
    head_flow, warp_inputs[0] = lax.optimization_barrier((head_flow, warp_inputs[0]))

    sc = ("strip", "chan")
    sc_sizes = (n_strip, n_chan)
    flow_slots = [jnp.zeros_like(head_flow) for _ in range(n_strip)]
    for k in range(n_strip * n_chan):
        if k == 0:
            got = head_flow
        else:
            got = shifted_from(head_flow, sc, sc_sizes, (k // n_chan, k % n_chan), cyclic=True)
        src_strip = (strip_index - k // n_chan) % n_strip
        for slot in range(n_strip):
            flow_slots[slot] = flow_slots[slot] + jnp.where(src_strip == slot, got, 0.0)
    flows_full = jnp.concatenate(flow_slots, axis=2) / n_chan

    base_terms = flows_full + q_full.astype(jnp.float32) * 0.125
    split = n_chan == 2
    if split:
        base_terms = lax.dynamic_slice_in_dim(base_terms, own_index, 1, 1)
    comps = base_terms.shape[1]

    def chain_local(incoming):
        src = incoming
        outs = []
        for local_sec in range(sec_local):
            src = base_terms[local_sec] + sample(
                jnp.pad(src, ((0, 0), (4, 4), (4, 4))), q_full[local_sec], 4
            )
            outs.append(src)
        return outs

    outs = chain_local(jnp.zeros((comps, total_rows, columns), jnp.float32))
    pending = list(range(1, len(pieces)))
    for turn in range(1, n_sec):
        carry = outs[-1]
        if pending:
            slot = pending.pop(0)
            carry, warp_inputs[slot] = lax.optimization_barrier((carry, warp_inputs[slot]))
        incoming = shifted_from(carry, ("sec",), (n_sec,), (1,))
        outs = chain_local(incoming)
    warped_pieces = [
        sample(jnp.pad(src, ((0, 0), (0, 0), (4, 4))), offsets[l], 4).astype(jnp.bfloat16)
        for src, (l, _, _) in zip(warp_inputs, pieces)
    ]
    warped = jnp.stack(
        [
            jnp.concatenate([w for w, p in zip(warped_pieces, pieces) if p[0] == l], axis=0)
            for l in range(sec_local)
        ]
    )
    composed = jnp.stack(
        [lax.dynamic_slice_in_dim(o, strip_first, strip_rows, 1) for o in outs]
    )
    if split:
        other = shifted_from(composed, ("chan",), (n_chan,), (1,), cyclic=True)
        composed = jnp.where(
            own_index == 0,
            jnp.concatenate([composed, other], axis=1),
            jnp.concatenate([other, composed], axis=1),
        )
    return (warped, composed)


def solution(mesh):
    in_specs = (
        P(("groups", "sec"), "strip", None),
        P(),
        P(),
        P(("groups", "sec"), None, "strip", None),
    )
    out_specs = (
        P(("groups", "sec"), "chan", "strip", None),
        P(("groups", "sec"), None, "strip", None),
    )
    return jax.shard_map(local, mesh=mesh, in_specs=in_specs, out_specs=out_specs, check_vma=False)
```

```python
import jax
import jax.numpy as jnp
from jax import lax
from jax.sharding import PartitionSpec as P

score_scale = 4.0


def shifted_from(value, axes, sizes, deltas, cyclic=False):
    pairs = []
    counts = [int(s) for s in sizes]
    total = 1
    for c in counts:
        total *= c
    for dst in range(total):
        coords = []
        rem = dst
        for c in reversed(counts):
            coords.append(rem % c)
            rem //= c
        coords = coords[::-1]
        src_coords = []
        ok = True
        for coord, c, d in zip(coords, counts, deltas):
            s = coord - d
            if cyclic:
                s %= c
            elif s < 0 or s >= c:
                ok = False
            src_coords.append(s)
        if not ok:
            continue
        src = 0
        for s, c in zip(src_coords, counts):
            src = src * c + s
        if src != dst:
            pairs.append((src, dst))
    if not pairs:
        return jnp.zeros_like(value)
    return lax.ppermute(value, axes if len(axes) > 1 else axes[0], pairs)


def first_taps(extended, rows_out, row_start):
    columns = extended.shape[-1]
    padded = jnp.pad(extended, ((0, 0), (0, 0), (2, 2)))
    tap_list = []
    for shift_y in (-2, 0, 2):
        for shift_x in (-2, 0, 2):
            tap_list.append(
                padded[
                    :,
                    row_start + shift_y : row_start + shift_y + rows_out,
                    2 + shift_x : 2 + shift_x + columns,
                ]
            )
    return jnp.stack(tap_list)


def second_terms(weights, inputs):
    rows_out = inputs.shape[2] - 2
    columns = inputs.shape[3]
    summed = None
    for shift_x in (-1, 0, 1):
        part = None
        for shift_y in (-1, 0, 1):
            tap_index = 3 * (shift_y + 1) + (shift_x + 1)
            window = inputs[:, :, 1 + shift_y : 1 + shift_y + rows_out, :]
            tap_term = jnp.einsum(
                "oi,ispw->ospw", weights[tap_index], window, preferred_element_type=jnp.float32
            )
            part = tap_term if part is None else part + tap_term
        if shift_x < 0:
            part = jnp.pad(part, ((0, 0), (0, 0), (0, 0), (1, 0)))[..., :columns]
        elif shift_x > 0:
            part = jnp.pad(part, ((0, 0), (0, 0), (0, 0), (0, 1)))[..., 1:]
        summed = part if summed is None else summed + part
    return summed


def hat_weights(quant_row):
    base = jnp.floor_divide(quant_row, 8)
    frac = (quant_row - 8 * base).astype(jnp.float32) * 0.125
    return [
        jnp.where(base == shift, 1.0 - frac, 0.0) + jnp.where(base + 1 == shift, frac, 0.0)
        for shift in range(-4, 5)
    ]


def sample(source, quant, row_start):
    rows_out, columns = (quant.shape[1], quant.shape[2])
    hats_y = hat_weights(quant[0])
    hats_x = hat_weights(quant[1])
    summed = jnp.zeros((source.shape[0], rows_out, columns), jnp.float32)
    for index_x in range(9):
        inner = jnp.zeros((source.shape[0], rows_out, columns), jnp.float32)
        for index_y in range(9):
            lower = row_start + index_y - 4
            window = source[:, lower : lower + rows_out, index_x : index_x + columns].astype(
                jnp.float32
            )
            inner = inner + hats_y[index_y] * window
        summed = summed + hats_x[index_x] * inner
    return summed


def local(sections, w_first, w_second, offsets):
    sec_local, strip_rows, columns = sections.shape
    n_sec = lax.axis_size("sec")
    n_strip = lax.axis_size("strip")
    n_chan = lax.axis_size("chan")
    strip_index = lax.axis_index("strip")
    own_index = lax.axis_index("chan")
    head_width = w_second.shape[1] // n_chan
    strip_first = strip_index * strip_rows
    total_rows = strip_rows * n_strip
    halo = 7
    ss = ("sec", "strip")
    ss_sizes = (n_sec, n_strip)

    if n_strip == 2:
        packed = jnp.concatenate(
            [sections[:, None].astype(jnp.float32), offsets.astype(jnp.float32)], axis=1
        ).astype(jnp.bfloat16)
        partner = shifted_from(packed, ("strip",), (n_strip,), (1,), cyclic=True)
        other_sec = partner[:, 0]
        from_left = jnp.where(strip_index == 1, other_sec[:, strip_rows - halo :], 0.0)
        from_right = jnp.where(strip_index == 0, other_sec[:, :halo], 0.0)
        other_q = partner[:, 1:].astype(jnp.int32)
        q_full = jnp.where(
            strip_index == 0,
            jnp.concatenate([offsets, other_q], axis=2),
            jnp.concatenate([other_q, offsets], axis=2),
        )
    else:
        from_left = shifted_from(sections[:, strip_rows - halo :], ("strip",), (n_strip,), (1,))
        from_right = shifted_from(sections[:, :halo], ("strip",), (n_strip,), (-1,))
        offset_parts = [offsets]
        for k in range(1, n_strip):
            offset_parts.append(shifted_from(offsets, ("strip",), (n_strip,), (k,), cyclic=True))
        offset_rows = []
        for slot in range(n_strip):
            piece = offset_parts[0]
            for k in range(1, n_strip):
                piece = jnp.where((strip_index - k) % n_strip == slot, offset_parts[k], piece)
            offset_rows.append(piece)
        q_full = jnp.concatenate(offset_rows, axis=2)
    own_ext = jnp.concatenate([from_left, sections, from_right], axis=1)
    prev_ext = shifted_from(own_ext[sec_local - 1 :], ("sec",), (n_sec,), (1,))

    first_rows = strip_rows + 10
    global_rows = strip_first - 5 + lax.broadcasted_iota(jnp.int32, (first_rows, 1), 0)
    inside = (global_rows >= 0) & (global_rows < total_rows)
    feat_rows = global_rows[1:-1]
    feat_inside = (feat_rows >= 0) & (feat_rows < total_rows)
    w_outputs = lax.dynamic_slice_in_dim(w_second, own_index * head_width, head_width, 1)
    w_taps = w_first.astype(jnp.float32)

    def features_of(ext):
        padded = jnp.pad(ext, ((0, 0), (0, 0), (2, 2))).astype(jnp.float32)
        windows = [
            padded[:, 2 + shift_y : 2 + shift_y + first_rows, 2 + shift_x : 2 + shift_x + columns]
            for shift_y in (-2, 0, 2)
            for shift_x in (-2, 0, 2)
        ]
        windows = lax.optimization_barrier(windows)
        maps = None
        for tap_index, window in enumerate(windows):
            term = w_taps[:, tap_index, None, None, None] * window[None]
            maps = term if maps is None else maps + term
        maps = jnp.where(inside, jnp.maximum(maps, 0.0), 0.0).astype(jnp.bfloat16)
        mixed = second_terms(w_outputs, maps)
        return jnp.where(feat_inside, jnp.maximum(mixed, 0.0), 0.0).astype(jnp.bfloat16)

    framed = features_of(jnp.concatenate([prev_ext, own_ext], axis=0))

    current = framed[:, 1:, 4 : 4 + strip_rows, :]
    earlier = jnp.pad(framed[:, :sec_local], ((0, 0), (0, 0), (0, 0), (4, 4)))
    factor = score_scale / head_width
    field_shape = (sec_local, strip_rows, columns)
    running_max = jnp.full(field_shape, -1e30, jnp.float32)
    weight_sum = jnp.zeros(field_shape, jnp.float32)
    along_y = jnp.zeros(field_shape, jnp.float32)
    along_x = jnp.zeros(field_shape, jnp.float32)
    step_cols = lax.broadcasted_iota(jnp.float32, (9, 1, 1, 1), 0) - 4.0
    for shift_y in range(9):
        scores = (
            jnp.stack(
                [
                    jnp.einsum(
                        "cspw,cspw->spw",
                        current,
                        earlier[:, :, shift_y : shift_y + strip_rows, shift_x : shift_x + columns],
                        preferred_element_type=jnp.float32,
                    )
                    for shift_x in range(9)
                ]
            )
            * factor
        )
        highest = jnp.maximum(running_max, jnp.max(scores, axis=0))
        rescale = jnp.exp(running_max - highest)
        weights = jnp.exp(scores - highest)
        block_sum = jnp.sum(weights, axis=0)
        weight_sum = weight_sum * rescale + block_sum
        along_y = along_y * rescale + (shift_y - 4.0) * block_sum
        along_x = along_x * rescale + jnp.sum(weights * step_cols, axis=0)
        running_max = highest
    head_flow = jnp.stack([along_y / weight_sum, along_x / weight_sum], axis=1)

    pieces = [(0, 0, head_width)]
    chain_slots = max(n_sec - 1, 1)
    rest = sec_local - 1
    per_sec = max(1, -(-chain_slots // max(rest, 1))) if rest else 0
    for local_sec in range(1, sec_local):
        bounds = [round(head_width * k / per_sec) for k in range(per_sec + 1)]
        for lo_c, hi_c in zip(bounds[:-1], bounds[1:]):
            pieces.append((local_sec, lo_c, hi_c))
    warp_inputs = [framed[lo_c:hi_c, l + 1] for l, lo_c, hi_c in pieces]
    head_flow, warp_inputs[0] = lax.optimization_barrier((head_flow, warp_inputs[0]))

    sc = ("strip", "chan")
    sc_sizes = (n_strip, n_chan)
    flow_slots = [jnp.zeros_like(head_flow) for _ in range(n_strip)]
    for k in range(n_strip * n_chan):
        if k == 0:
            got = head_flow
        else:
            got = shifted_from(head_flow, sc, sc_sizes, (k // n_chan, k % n_chan), cyclic=True)
        src_strip = (strip_index - k // n_chan) % n_strip
        for slot in range(n_strip):
            flow_slots[slot] = flow_slots[slot] + jnp.where(src_strip == slot, got, 0.0)
    flows_full = jnp.concatenate(flow_slots, axis=2) / n_chan

    base_terms = flows_full + q_full.astype(jnp.float32) * 0.125
    split = n_chan == 2
    if split:
        base_terms = lax.dynamic_slice_in_dim(base_terms, own_index, 1, 1)
    comps = base_terms.shape[1]

    def chain_local(incoming):
        src = incoming
        outs = []
        for local_sec in range(sec_local):
            src = base_terms[local_sec] + sample(
                jnp.pad(src, ((0, 0), (4, 4), (4, 4))), q_full[local_sec], 4
            )
            outs.append(src)
        return outs

    outs = chain_local(jnp.zeros((comps, total_rows, columns), jnp.float32))
    pending = list(range(1, len(pieces)))
    for turn in range(1, n_sec):
        carry = outs[-1]
        if pending:
            slot = pending.pop(0)
            carry, warp_inputs[slot] = lax.optimization_barrier((carry, warp_inputs[slot]))
        incoming = shifted_from(carry, ("sec",), (n_sec,), (1,))
        outs = chain_local(incoming)
    warped_pieces = [
        sample(jnp.pad(src, ((0, 0), (0, 0), (4, 4))), offsets[l], 4).astype(jnp.bfloat16)
        for src, (l, _, _) in zip(warp_inputs, pieces)
    ]
    warped = jnp.stack(
        [
            jnp.concatenate([w for w, p in zip(warped_pieces, pieces) if p[0] == l], axis=0)
            for l in range(sec_local)
        ]
    )
    composed = jnp.stack(
        [lax.dynamic_slice_in_dim(o, strip_first, strip_rows, 1) for o in outs]
    )
    if split:
        other = shifted_from(composed, ("chan",), (n_chan,), (1,), cyclic=True)
        composed = jnp.where(
            own_index == 0,
            jnp.concatenate([composed, other], axis=1),
            jnp.concatenate([other, composed], axis=1),
        )
    return (warped, composed)


def solution(mesh):
    in_specs = (
        P(("groups", "sec"), "strip", None),
        P(),
        P(),
        P(("groups", "sec"), None, "strip", None),
    )
    out_specs = (
        P(("groups", "sec"), "chan", "strip", None),
        P(("groups", "sec"), None, "strip", None),
    )
    return jax.shard_map(local, mesh=mesh, in_specs=in_specs, out_specs=out_specs, check_vma=False)
```

```python
import jax
import jax.numpy as jnp
from jax import lax
from jax.sharding import PartitionSpec as P

score_scale = 4.0


def shifted_from(value, axes, sizes, deltas, cyclic=False):
    pairs = []
    counts = [int(s) for s in sizes]
    total = 1
    for c in counts:
        total *= c
    for dst in range(total):
        coords = []
        rem = dst
        for c in reversed(counts):
            coords.append(rem % c)
            rem //= c
        coords = coords[::-1]
        src_coords = []
        ok = True
        for coord, c, d in zip(coords, counts, deltas):
            s = coord - d
            if cyclic:
                s %= c
            elif s < 0 or s >= c:
                ok = False
            src_coords.append(s)
        if not ok:
            continue
        src = 0
        for s, c in zip(src_coords, counts):
            src = src * c + s
        if src != dst:
            pairs.append((src, dst))
    if not pairs:
        return jnp.zeros_like(value)
    return lax.ppermute(value, axes if len(axes) > 1 else axes[0], pairs)


def first_taps(extended, rows_out, row_start):
    columns = extended.shape[-1]
    padded = jnp.pad(extended, ((0, 0), (0, 0), (2, 2)))
    tap_list = []
    for shift_y in (-2, 0, 2):
        for shift_x in (-2, 0, 2):
            tap_list.append(
                padded[
                    :,
                    row_start + shift_y : row_start + shift_y + rows_out,
                    2 + shift_x : 2 + shift_x + columns,
                ]
            )
    return jnp.stack(tap_list)


def second_terms(weights, inputs):
    rows_out = inputs.shape[2] - 2
    columns = inputs.shape[3]
    summed = None
    for shift_x in (-1, 0, 1):
        part = None
        for shift_y in (-1, 0, 1):
            tap_index = 3 * (shift_y + 1) + (shift_x + 1)
            window = inputs[:, :, 1 + shift_y : 1 + shift_y + rows_out, :]
            tap_term = jnp.einsum(
                "oi,ispw->ospw", weights[tap_index], window, preferred_element_type=jnp.float32
            )
            part = tap_term if part is None else part + tap_term
        if shift_x < 0:
            part = jnp.pad(part, ((0, 0), (0, 0), (0, 0), (1, 0)))[..., :columns]
        elif shift_x > 0:
            part = jnp.pad(part, ((0, 0), (0, 0), (0, 0), (0, 1)))[..., 1:]
        summed = part if summed is None else summed + part
    return summed


def hat_weights(quant_row):
    base = jnp.floor_divide(quant_row, 8)
    frac = (quant_row - 8 * base).astype(jnp.float32) * 0.125
    return [
        jnp.where(base == shift, 1.0 - frac, 0.0) + jnp.where(base + 1 == shift, frac, 0.0)
        for shift in range(-4, 5)
    ]


def sample(source, quant, row_start):
    rows_out, columns = (quant.shape[1], quant.shape[2])
    hats_y = hat_weights(quant[0])
    hats_x = hat_weights(quant[1])
    summed = jnp.zeros((source.shape[0], rows_out, columns), jnp.float32)
    for index_x in range(9):
        inner = jnp.zeros((source.shape[0], rows_out, columns), jnp.float32)
        for index_y in range(9):
            lower = row_start + index_y - 4
            window = source[:, lower : lower + rows_out, index_x : index_x + columns].astype(
                jnp.float32
            )
            inner = inner + hats_y[index_y] * window
        summed = summed + hats_x[index_x] * inner
    return summed


def local(sections, w_first, w_second, offsets):
    sec_local, strip_rows, columns = sections.shape
    n_sec = lax.axis_size("sec")
    n_strip = lax.axis_size("strip")
    n_chan = lax.axis_size("chan")
    strip_index = lax.axis_index("strip")
    own_index = lax.axis_index("chan")
    head_width = w_second.shape[1] // n_chan
    strip_first = strip_index * strip_rows
    total_rows = strip_rows * n_strip
    halo = 7
    ss = ("sec", "strip")
    ss_sizes = (n_sec, n_strip)

    if n_strip == 2:
        packed = jnp.concatenate(
            [sections[:, None].astype(jnp.float32), offsets.astype(jnp.float32)], axis=1
        ).astype(jnp.bfloat16)
        partner = shifted_from(packed, ("strip",), (n_strip,), (1,), cyclic=True)
        other_sec = partner[:, 0]
        from_left = jnp.where(strip_index == 1, other_sec[:, strip_rows - halo :], 0.0)
        from_right = jnp.where(strip_index == 0, other_sec[:, :halo], 0.0)
        other_q = partner[:, 1:].astype(jnp.int32)
        q_full = jnp.where(
            strip_index == 0,
            jnp.concatenate([offsets, other_q], axis=2),
            jnp.concatenate([other_q, offsets], axis=2),
        )
    else:
        from_left = shifted_from(sections[:, strip_rows - halo :], ("strip",), (n_strip,), (1,))
        from_right = shifted_from(sections[:, :halo], ("strip",), (n_strip,), (-1,))
        offset_parts = [offsets]
        for k in range(1, n_strip):
            offset_parts.append(shifted_from(offsets, ("strip",), (n_strip,), (k,), cyclic=True))
        offset_rows = []
        for slot in range(n_strip):
            piece = offset_parts[0]
            for k in range(1, n_strip):
                piece = jnp.where((strip_index - k) % n_strip == slot, offset_parts[k], piece)
            offset_rows.append(piece)
        q_full = jnp.concatenate(offset_rows, axis=2)
    own_ext = jnp.concatenate([from_left, sections, from_right], axis=1)
    prev_ext = shifted_from(own_ext[sec_local - 1 :], ("sec",), (n_sec,), (1,))

    first_rows = strip_rows + 10
    global_rows = strip_first - 5 + lax.broadcasted_iota(jnp.int32, (first_rows, 1), 0)
    inside = (global_rows >= 0) & (global_rows < total_rows)
    feat_rows = global_rows[1:-1]
    feat_inside = (feat_rows >= 0) & (feat_rows < total_rows)
    w_outputs = lax.dynamic_slice_in_dim(w_second, own_index * head_width, head_width, 1)
    w_taps = w_first.astype(jnp.float32)

    def features_of(ext):
        padded = jnp.pad(ext, ((0, 0), (0, 0), (2, 2))).astype(jnp.float32)
        windows = [
            padded[:, 2 + shift_y : 2 + shift_y + first_rows, 2 + shift_x : 2 + shift_x + columns]
            for shift_y in (-2, 0, 2)
            for shift_x in (-2, 0, 2)
        ]
        windows = lax.optimization_barrier(windows)
        maps = None
        for tap_index, window in enumerate(windows):
            term = w_taps[:, tap_index, None, None, None] * window[None]
            maps = term if maps is None else maps + term
        maps = jnp.where(inside, jnp.maximum(maps, 0.0), 0.0).astype(jnp.bfloat16)
        mixed = second_terms(w_outputs, maps)
        return jnp.where(feat_inside, jnp.maximum(mixed, 0.0), 0.0).astype(jnp.bfloat16)

    framed = features_of(jnp.concatenate([prev_ext, own_ext], axis=0))

    current = framed[:, 1:, 4 : 4 + strip_rows, :]
    earlier = framed[:, :sec_local]
    cur_shift = []
    for shift_x in range(9):
        disp = shift_x - 4
        if disp > 0:
            cur_shift.append(jnp.pad(current, ((0, 0), (0, 0), (0, 0), (disp, 0)))[..., :columns])
        elif disp < 0:
            cur_shift.append(jnp.pad(current, ((0, 0), (0, 0), (0, 0), (0, -disp)))[..., -disp:])
        else:
            cur_shift.append(current)
    cur_shift = lax.optimization_barrier(cur_shift)

    def shifted_score(shift_x, rows):
        disp = shift_x - 4
        part = jnp.einsum("cspw,cspw->spw", cur_shift[shift_x], rows, preferred_element_type=jnp.float32)
        if disp > 0:
            return jnp.pad(part, ((0, 0), (0, 0), (0, disp)))[..., disp:]
        if disp < 0:
            return jnp.pad(part, ((0, 0), (0, 0), (-disp, 0)))[..., :columns]
        return part

    factor = score_scale / head_width
    field_shape = (sec_local, strip_rows, columns)
    running_max = jnp.full(field_shape, -1e30, jnp.float32)
    weight_sum = jnp.zeros(field_shape, jnp.float32)
    along_y = jnp.zeros(field_shape, jnp.float32)
    along_x = jnp.zeros(field_shape, jnp.float32)
    step_cols = lax.broadcasted_iota(jnp.float32, (9, 1, 1, 1), 0) - 4.0
    for shift_y in range(9):
        rows = earlier[:, :, shift_y : shift_y + strip_rows, :]
        scores = jnp.stack([shifted_score(shift_x, rows) for shift_x in range(9)]) * factor
        highest = jnp.maximum(running_max, jnp.max(scores, axis=0))
        rescale = jnp.exp(running_max - highest)
        weights = jnp.exp(scores - highest)
        block_sum = jnp.sum(weights, axis=0)
        weight_sum = weight_sum * rescale + block_sum
        along_y = along_y * rescale + (shift_y - 4.0) * block_sum
        along_x = along_x * rescale + jnp.sum(weights * step_cols, axis=0)
        running_max = highest
    head_flow = jnp.stack([along_y / weight_sum, along_x / weight_sum], axis=1)

    pieces = [(0, 0, head_width)]
    chain_slots = max(n_sec - 1, 1)
    rest = sec_local - 1
    per_sec = max(1, -(-chain_slots // max(rest, 1))) if rest else 0
    for local_sec in range(1, sec_local):
        bounds = [round(head_width * k / per_sec) for k in range(per_sec + 1)]
        for lo_c, hi_c in zip(bounds[:-1], bounds[1:]):
            pieces.append((local_sec, lo_c, hi_c))
    warp_inputs = [framed[lo_c:hi_c, l + 1] for l, lo_c, hi_c in pieces]
    head_flow, warp_inputs[0] = lax.optimization_barrier((head_flow, warp_inputs[0]))

    sc = ("strip", "chan")
    sc_sizes = (n_strip, n_chan)
    flow_slots = [jnp.zeros_like(head_flow) for _ in range(n_strip)]
    for k in range(n_strip * n_chan):
        if k == 0:
            got = head_flow
        else:
            got = shifted_from(head_flow, sc, sc_sizes, (k // n_chan, k % n_chan), cyclic=True)
        src_strip = (strip_index - k // n_chan) % n_strip
        for slot in range(n_strip):
            flow_slots[slot] = flow_slots[slot] + jnp.where(src_strip == slot, got, 0.0)
    flows_full = jnp.concatenate(flow_slots, axis=2) / n_chan

    base_terms = flows_full + q_full.astype(jnp.float32) * 0.125
    split = n_chan == 2
    if split:
        base_terms = lax.dynamic_slice_in_dim(base_terms, own_index, 1, 1)
    comps = base_terms.shape[1]

    def chain_local(incoming):
        src = incoming
        outs = []
        for local_sec in range(sec_local):
            src = base_terms[local_sec] + sample(
                jnp.pad(src, ((0, 0), (4, 4), (4, 4))), q_full[local_sec], 4
            )
            outs.append(src)
        return outs

    outs = chain_local(jnp.zeros((comps, total_rows, columns), jnp.float32))
    pending = list(range(1, len(pieces)))
    for turn in range(1, n_sec):
        carry = outs[-1]
        if pending:
            slot = pending.pop(0)
            carry, warp_inputs[slot] = lax.optimization_barrier((carry, warp_inputs[slot]))
        incoming = shifted_from(carry, ("sec",), (n_sec,), (1,))
        outs = chain_local(incoming)
    warped_pieces = [
        sample(jnp.pad(src, ((0, 0), (0, 0), (4, 4))), offsets[l], 4).astype(jnp.bfloat16)
        for src, (l, _, _) in zip(warp_inputs, pieces)
    ]
    warped = jnp.stack(
        [
            jnp.concatenate([w for w, p in zip(warped_pieces, pieces) if p[0] == l], axis=0)
            for l in range(sec_local)
        ]
    )
    composed = jnp.stack(
        [lax.dynamic_slice_in_dim(o, strip_first, strip_rows, 1) for o in outs]
    )
    if split:
        other = shifted_from(composed, ("chan",), (n_chan,), (1,), cyclic=True)
        composed = jnp.where(
            own_index == 0,
            jnp.concatenate([composed, other], axis=1),
            jnp.concatenate([other, composed], axis=1),
        )
    return (warped, composed)


def solution(mesh):
    in_specs = (
        P(("groups", "sec"), "strip", None),
        P(),
        P(),
        P(("groups", "sec"), None, "strip", None),
    )
    out_specs = (
        P(("groups", "sec"), "chan", "strip", None),
        P(("groups", "sec"), None, "strip", None),
    )
    return jax.shard_map(local, mesh=mesh, in_specs=in_specs, out_specs=out_specs, check_vma=False)
```

```python
import jax
import jax.numpy as jnp
from jax import lax
from jax.sharding import PartitionSpec as P

score_scale = 4.0


def shifted_from(value, axes, sizes, deltas, cyclic=False):
    pairs = []
    counts = [int(s) for s in sizes]
    total = 1
    for c in counts:
        total *= c
    for dst in range(total):
        coords = []
        rem = dst
        for c in reversed(counts):
            coords.append(rem % c)
            rem //= c
        coords = coords[::-1]
        src_coords = []
        ok = True
        for coord, c, d in zip(coords, counts, deltas):
            s = coord - d
            if cyclic:
                s %= c
            elif s < 0 or s >= c:
                ok = False
            src_coords.append(s)
        if not ok:
            continue
        src = 0
        for s, c in zip(src_coords, counts):
            src = src * c + s
        if src != dst:
            pairs.append((src, dst))
    if not pairs:
        return jnp.zeros_like(value)
    return lax.ppermute(value, axes if len(axes) > 1 else axes[0], pairs)


def first_taps(extended, rows_out, row_start):
    columns = extended.shape[-1]
    padded = jnp.pad(extended, ((0, 0), (0, 0), (2, 2)))
    tap_list = []
    for shift_y in (-2, 0, 2):
        for shift_x in (-2, 0, 2):
            tap_list.append(
                padded[
                    :,
                    row_start + shift_y : row_start + shift_y + rows_out,
                    2 + shift_x : 2 + shift_x + columns,
                ]
            )
    return jnp.stack(tap_list)


def second_terms(weights, inputs):
    rows_out = inputs.shape[2] - 2
    columns = inputs.shape[3]
    summed = None
    for shift_x in (-1, 0, 1):
        part = None
        for shift_y in (-1, 0, 1):
            tap_index = 3 * (shift_y + 1) + (shift_x + 1)
            window = inputs[:, :, 1 + shift_y : 1 + shift_y + rows_out, :]
            tap_term = jnp.einsum(
                "oi,ispw->ospw", weights[tap_index], window, preferred_element_type=jnp.float32
            )
            part = tap_term if part is None else part + tap_term
        if shift_x < 0:
            part = jnp.pad(part, ((0, 0), (0, 0), (0, 0), (1, 0)))[..., :columns]
        elif shift_x > 0:
            part = jnp.pad(part, ((0, 0), (0, 0), (0, 0), (0, 1)))[..., 1:]
        summed = part if summed is None else summed + part
    return summed


def hat_weights(quant_row):
    base = jnp.floor_divide(quant_row, 8)
    frac = (quant_row - 8 * base).astype(jnp.float32) * 0.125
    return [
        jnp.where(base == shift, 1.0 - frac, 0.0) + jnp.where(base + 1 == shift, frac, 0.0)
        for shift in range(-4, 5)
    ]


def sample(source, quant, row_start):
    rows_out, columns = (quant.shape[1], quant.shape[2])
    hats_y = hat_weights(quant[0])
    hats_x = hat_weights(quant[1])
    summed = jnp.zeros((source.shape[0], rows_out, columns), jnp.float32)
    for index_x in range(9):
        inner = jnp.zeros((source.shape[0], rows_out, columns), jnp.float32)
        for index_y in range(9):
            lower = row_start + index_y - 4
            window = source[:, lower : lower + rows_out, index_x : index_x + columns].astype(
                jnp.float32
            )
            inner = inner + hats_y[index_y] * window
        summed = summed + hats_x[index_x] * inner
    return summed


def take_cols(x, disp):
    columns = x.shape[-1]
    widths = [(0, 0)] * (x.ndim - 1)
    if disp > 0:
        return jnp.pad(x, widths + [(0, disp)])[..., disp : disp + columns]
    if disp < 0:
        return jnp.pad(x, widths + [(-disp, 0)])[..., :columns]
    return x


def sample_aligned(source, quant, row_start):
    rows_out, columns = (quant.shape[1], quant.shape[2])
    hats_x = hat_weights(quant[1])
    summed = jnp.zeros((source.shape[0], rows_out, columns), jnp.float32)
    for index_x in range(9):
        disp = index_x - 4
        hats_y = hat_weights(take_cols(quant[0], -disp))
        inner = jnp.zeros((source.shape[0], rows_out, columns), jnp.float32)
        for index_y in range(9):
            lower = row_start + index_y - 4
            window = source[:, lower : lower + rows_out, :].astype(jnp.float32)
            inner = inner + hats_y[index_y] * window
        summed = summed + hats_x[index_x] * take_cols(inner, disp)
    return summed


def local(sections, w_first, w_second, offsets):
    sec_local, strip_rows, columns = sections.shape
    n_sec = lax.axis_size("sec")
    n_strip = lax.axis_size("strip")
    n_chan = lax.axis_size("chan")
    strip_index = lax.axis_index("strip")
    own_index = lax.axis_index("chan")
    head_width = w_second.shape[1] // n_chan
    strip_first = strip_index * strip_rows
    total_rows = strip_rows * n_strip
    halo = 7
    ss = ("sec", "strip")
    ss_sizes = (n_sec, n_strip)

    if n_strip == 2:
        packed = jnp.concatenate(
            [sections[:, None].astype(jnp.float32), offsets.astype(jnp.float32)], axis=1
        ).astype(jnp.bfloat16)
        partner = shifted_from(packed, ("strip",), (n_strip,), (1,), cyclic=True)
        other_sec = partner[:, 0]
        from_left = jnp.where(strip_index == 1, other_sec[:, strip_rows - halo :], 0.0)
        from_right = jnp.where(strip_index == 0, other_sec[:, :halo], 0.0)
        other_q = partner[:, 1:].astype(jnp.int32)
        q_full = jnp.where(
            strip_index == 0,
            jnp.concatenate([offsets, other_q], axis=2),
            jnp.concatenate([other_q, offsets], axis=2),
        )
    else:
        from_left = shifted_from(sections[:, strip_rows - halo :], ("strip",), (n_strip,), (1,))
        from_right = shifted_from(sections[:, :halo], ("strip",), (n_strip,), (-1,))
        offset_parts = [offsets]
        for k in range(1, n_strip):
            offset_parts.append(shifted_from(offsets, ("strip",), (n_strip,), (k,), cyclic=True))
        offset_rows = []
        for slot in range(n_strip):
            piece = offset_parts[0]
            for k in range(1, n_strip):
                piece = jnp.where((strip_index - k) % n_strip == slot, offset_parts[k], piece)
            offset_rows.append(piece)
        q_full = jnp.concatenate(offset_rows, axis=2)
    own_ext = jnp.concatenate([from_left, sections, from_right], axis=1)
    prev_ext = shifted_from(own_ext[sec_local - 1 :], ("sec",), (n_sec,), (1,))

    first_rows = strip_rows + 10
    global_rows = strip_first - 5 + lax.broadcasted_iota(jnp.int32, (first_rows, 1), 0)
    inside = (global_rows >= 0) & (global_rows < total_rows)
    feat_rows = global_rows[1:-1]
    feat_inside = (feat_rows >= 0) & (feat_rows < total_rows)
    w_outputs = lax.dynamic_slice_in_dim(w_second, own_index * head_width, head_width, 1)
    w_taps = w_first.astype(jnp.float32)

    def features_of(ext):
        padded = jnp.pad(ext, ((0, 0), (0, 0), (2, 2))).astype(jnp.float32)
        windows = [
            padded[:, 2 + shift_y : 2 + shift_y + first_rows, 2 + shift_x : 2 + shift_x + columns]
            for shift_y in (-2, 0, 2)
            for shift_x in (-2, 0, 2)
        ]
        windows = lax.optimization_barrier(windows)
        maps = None
        for tap_index, window in enumerate(windows):
            term = w_taps[:, tap_index, None, None, None] * window[None]
            maps = term if maps is None else maps + term
        maps = jnp.where(inside, jnp.maximum(maps, 0.0), 0.0).astype(jnp.bfloat16)
        mixed = second_terms(w_outputs, maps)
        return jnp.where(feat_inside, jnp.maximum(mixed, 0.0), 0.0).astype(jnp.bfloat16)

    framed = features_of(jnp.concatenate([prev_ext, own_ext], axis=0))

    current = framed[:, 1:, 4 : 4 + strip_rows, :]
    earlier = jnp.pad(framed[:, :sec_local], ((0, 0), (0, 0), (0, 0), (4, 4)))
    factor = score_scale / head_width
    field_shape = (sec_local, strip_rows, columns)
    running_max = jnp.full(field_shape, -1e30, jnp.float32)
    weight_sum = jnp.zeros(field_shape, jnp.float32)
    along_y = jnp.zeros(field_shape, jnp.float32)
    along_x = jnp.zeros(field_shape, jnp.float32)
    step_cols = lax.broadcasted_iota(jnp.float32, (9, 1, 1, 1), 0) - 4.0
    for shift_y in range(9):
        scores = (
            jnp.stack(
                [
                    jnp.einsum(
                        "cspw,cspw->spw",
                        current,
                        earlier[:, :, shift_y : shift_y + strip_rows, shift_x : shift_x + columns],
                        preferred_element_type=jnp.float32,
                    )
                    for shift_x in range(9)
                ]
            )
            * factor
        )
        highest = jnp.maximum(running_max, jnp.max(scores, axis=0))
        rescale = jnp.exp(running_max - highest)
        weights = jnp.exp(scores - highest)
        block_sum = jnp.sum(weights, axis=0)
        weight_sum = weight_sum * rescale + block_sum
        along_y = along_y * rescale + (shift_y - 4.0) * block_sum
        along_x = along_x * rescale + jnp.sum(weights * step_cols, axis=0)
        running_max = highest
    head_flow = jnp.stack([along_y / weight_sum, along_x / weight_sum], axis=1)

    pieces = [(0, 0, head_width)]
    chain_slots = max(n_sec - 1, 1)
    rest = sec_local - 1
    per_sec = max(1, -(-chain_slots // max(rest, 1))) if rest else 0
    for local_sec in range(1, sec_local):
        bounds = [round(head_width * k / per_sec) for k in range(per_sec + 1)]
        for lo_c, hi_c in zip(bounds[:-1], bounds[1:]):
            pieces.append((local_sec, lo_c, hi_c))
    warp_inputs = [framed[lo_c:hi_c, l + 1] for l, lo_c, hi_c in pieces]
    head_flow, warp_inputs[0] = lax.optimization_barrier((head_flow, warp_inputs[0]))

    sc = ("strip", "chan")
    sc_sizes = (n_strip, n_chan)
    flow_slots = [jnp.zeros_like(head_flow) for _ in range(n_strip)]
    for k in range(n_strip * n_chan):
        if k == 0:
            got = head_flow
        else:
            got = shifted_from(head_flow, sc, sc_sizes, (k // n_chan, k % n_chan), cyclic=True)
        src_strip = (strip_index - k // n_chan) % n_strip
        for slot in range(n_strip):
            flow_slots[slot] = flow_slots[slot] + jnp.where(src_strip == slot, got, 0.0)
    flows_full = jnp.concatenate(flow_slots, axis=2) / n_chan

    base_terms = flows_full + q_full.astype(jnp.float32) * 0.125
    split = n_chan == 2
    if split:
        base_terms = lax.dynamic_slice_in_dim(base_terms, own_index, 1, 1)
    comps = base_terms.shape[1]

    def chain_local(incoming):
        src = incoming
        outs = []
        for local_sec in range(sec_local):
            src = base_terms[local_sec] + sample(
                jnp.pad(src, ((0, 0), (4, 4), (4, 4))), q_full[local_sec], 4
            )
            outs.append(src)
        return outs

    outs = chain_local(jnp.zeros((comps, total_rows, columns), jnp.float32))
    pending = list(range(1, len(pieces)))
    for turn in range(1, n_sec):
        carry = outs[-1]
        if pending:
            slot = pending.pop(0)
            carry, warp_inputs[slot] = lax.optimization_barrier((carry, warp_inputs[slot]))
        incoming = shifted_from(carry, ("sec",), (n_sec,), (1,))
        outs = chain_local(incoming)
    warped_pieces = [
        sample_aligned(src, offsets[l], 4).astype(jnp.bfloat16)
        for src, (l, _, _) in zip(warp_inputs, pieces)
    ]
    warped = jnp.stack(
        [
            jnp.concatenate([w for w, p in zip(warped_pieces, pieces) if p[0] == l], axis=0)
            for l in range(sec_local)
        ]
    )
    composed = jnp.stack(
        [lax.dynamic_slice_in_dim(o, strip_first, strip_rows, 1) for o in outs]
    )
    if split:
        other = shifted_from(composed, ("chan",), (n_chan,), (1,), cyclic=True)
        composed = jnp.where(
            own_index == 0,
            jnp.concatenate([composed, other], axis=1),
            jnp.concatenate([other, composed], axis=1),
        )
    return (warped, composed)


def solution(mesh):
    in_specs = (
        P(("groups", "sec"), "strip", None),
        P(),
        P(),
        P(("groups", "sec"), None, "strip", None),
    )
    out_specs = (
        P(("groups", "sec"), "chan", "strip", None),
        P(("groups", "sec"), None, "strip", None),
    )
    return jax.shard_map(local, mesh=mesh, in_specs=in_specs, out_specs=out_specs, check_vma=False)
```
